32 devices in a mesh: req: 4 (over y, x), cand: 8 (over z, core).
Axes of the slice: x: 2, y: 2, z: 4, core: 2. Of those that a mesh axis runs over, the one named last changes fastest.
Arguments:
- table: bfloat16 [32768, 256], P('req'), may hold values from -6 to 6
- history_shard: int32 [4, 1024, 1], P('req', 'cand'), may hold values from 0 to 3; in each aligned block of 128 rows (0 to 127, 128 to 255, ..., all dimensions but the last counted through in order) at most 128 rows name the same one
- history_row: int32 [4, 1024], P('req', 'cand'), may hold values from 0 to 8191
- candidate_shard: int32 [4, 2048, 1], P('req', 'cand'), may hold values from 0 to 3; in each aligned block of 256 rows (0 to 255, 256 to 511, ..., all dimensions but the last counted through in order) at most 192 rows name the same one
- candidate_row: int32 [4, 2048], P('req', 'cand'), may hold values from 0 to 8191
- history_length: int32 [4], P('req'), may hold values from 128 to 1024, as said below
- w_query: bfloat16 [256, 256], replicated, may hold values from -0.375 to 0.375
- w_key: bfloat16 [256, 256], replicated, may hold values from -0.375 to 0.375
- w_value: bfloat16 [256, 256], replicated, may hold values from -0.375 to 0.375
- tower_in: bfloat16 [512, 1024], replicated, may hold values from -0.25 to 0.25
- tower_out: bfloat16 [1024], replicated, may hold values from -0.1875 to 0.1875
Outputs:
- logits: float32 [4, 2048], P('req', 'cand')
The draws below stay inside these ranges and needn't reach their ends.
Inputs may be any that keep to these rules, and one draw needn't show every extreme that they name: `history_shard`: among the 128 events of one request that one device holds, at most 128 name the same table shard, a bound that some block reaches. `candidate_shard`: among the 256 candidates of one request that one device holds, at most 192 name the same table shard, a bound that some block reaches. `history_length`: some request has all 1024 events live.
All inputs are finite; a program needn't handle non-finite values.
Results may differ from the reference program's by a relative error of at most 0.004.
Values may be sent and summed in bfloat16 or wider, within the bound.
No kernel may reach another device: no remote copies, remote signals or barrier semaphores. Data moves between devices by JAX's collectives and lax.ppermute only.
A program may use at most 64 MiB of HBM per device.

```python
import math
import jax
import jax.numpy as jnp
import numpy as np
from jax import lax

D = 256
HEADS = 4
TOWER = 1024
ROWS_DEV = 8192
HIST_DEV = 128
CAND_DEV = 256
REQS = 4
HIST = 1024
CANDS = 2048
TABLE = 32768
HCAP = 128
CCAP = 192
N_REQ = 4


def draw_history_length(key, part):
    first_key, second_key = jax.random.split(key)
    drawn = jax.random.randint(first_key, (REQS,), HIST // 8, HIST + 1)
    chosen = jax.random.randint(second_key, (), 0, REQS)
    return jnp.where(jnp.arange(REQS) == chosen, HIST, drawn).astype(jnp.int32)


def place_ends(entries, stream_key, smallest, largest):
    place = [jax.random.randint(jax.random.fold_in(stream_key, axis), (), 0, length) for axis, length in enumerate(entries.shape)]
    longest = entries.shape.index(max(entries.shape))
    neighbour = place[:longest] + [(place[longest] + 1) % entries.shape[longest]] + place[longest + 1:]
    return entries.at[tuple(place)].set(smallest).at[tuple(neighbour)].set(largest)


def shard_levels(own_key, dims, cuts, least, top_value):
    factor_of, own = 1.0, jax.random.fold_in(own_key, 6)
    for axis_at, shards_of in cuts:
        draws = jnp.exp(jax.random.uniform(jax.random.fold_in(own, axis_at), (shards_of,), jnp.float32, least / len(cuts), top_value / len(cuts)))
        factor_of = factor_of * jnp.repeat(draws, dims[axis_at] // shards_of).reshape([-1 if axis == axis_at else 1 for axis in range(len(dims))])
    return factor_of


def routed_block(rng, own, number, rows, amount, top, limit, slope):
    sequence = jax.random.permutation(rng, amount)
    heavy_load, usual = load_shares(amount, rows * top, limit, slope, True), load_shares(amount, rows * top, limit, slope, False)
    places = jnp.arange(amount)

    def named(sizes, offset_by):
        used = int((sizes > 0).sum())
        fixed = max(1, used // 4)
        moved = fixed + (places - fixed + offset_by * (used - fixed)) % max(1, amount - fixed)
        return jnp.zeros((amount,), jnp.int32).at[sequence[jnp.where(places < fixed, places, moved)]].set(jnp.asarray(sizes, jnp.int32))

    sizes = jnp.where(number % 4 == 0, named(heavy_load, number // 4), named(usual, number - number // 4 - 1))
    mixed = jax.random.permutation(jax.random.fold_in(own, 3), amount)
    donor, taker = mixed[0:amount // 2 * 2:2], mixed[1:amount // 2 * 2:2]
    margin = jnp.minimum(sizes[donor] - 1, limit - sizes[taker]) // 2
    margin = jnp.where((donor == sequence[0]) | (taker == sequence[0]) | (sizes[taker] == 0), 0, jnp.maximum(margin, 0))
    moved = jax.random.randint(jax.random.fold_in(own, 4), (amount // 2,), 0, 1 << 20) % (margin + 1)
    sizes = sizes.at[donor].add(-moved).at[taker].add(moved)
    members = jnp.searchsorted(jnp.cumsum(sizes), jnp.arange(rows * top), side="right").astype(jnp.int32)
    listing = members.reshape(top, rows).T
    listing = listing[jax.random.permutation(jax.random.fold_in(own, 1), rows)]
    offset_by = jax.random.randint(jax.random.fold_in(own, 2), (rows, 1), 0, top)
    return jnp.take_along_axis(listing, (jnp.arange(top)[None, :] + offset_by) % top, axis=1)


def load_shares(amount, total, bound, skew, full):
    weights = [(1 << 20) // math.isqrt(grade ** skew) + 1 for grade in range(1, amount + 1)]
    largest = bound if full else min(bound, max(-(-total // amount), total * weights[0] // sum(weights)))
    least = 1 if total - largest >= amount - 1 else 0
    holding, rest = [largest] + [least] * (amount - 1), total - largest - least * (amount - 1)
    while rest > 0:
        movable = [i for i in range(1, amount) if holding[i] < largest] or [i for i in range(1, amount) if holding[i] < bound]
        pool, remaining = sum([weights[i] for i in movable]), rest
        for i in movable:
            addition = min(bound - holding[i], max(1, remaining * weights[i] // pool), rest)
            holding[i] = holding[i] + addition
            rest = rest - addition
    return np.array(holding)


def gaussian(stream_key, shape, scale, bound, shards=(), held_as=jnp.bfloat16):
    gain = shard_levels(stream_key, shape, shards, -0.22, 0.18) if shards else 1.0
    values = jax.random.normal(stream_key, shape, jnp.float32) * scale * gain
    return jnp.minimum(jnp.maximum(values, -bound), bound).astype(held_as)


def setup_inputs(seed: int = 0) -> dict:
    streams_of = jax.random.split(jax.random.key(seed), 12)
    table = gaussian(streams_of[0], (TABLE, D), 1.0, 6.0, ((0, 4),))
    history_shard_keys = jax.random.split(jax.random.fold_in(streams_of[1], 1), REQS * HIST // HIST_DEV)
    history_shard_turns = jax.random.permutation(jax.random.fold_in(streams_of[1], 3), REQS * HIST // HIST_DEV)
    history_shard = jax.vmap(lambda own, number: routed_block(jax.random.fold_in(streams_of[1], 2), own, number, HIST_DEV, N_REQ, 1, HCAP, 2))(history_shard_keys, history_shard_turns).reshape((REQS, HIST, 1))
    history_row = place_ends(jax.random.randint(streams_of[2], (REQS, HIST), 0, ROWS_DEV), jax.random.fold_in(streams_of[2], 1), 0, ROWS_DEV - 1).astype(jnp.int32)
    candidate_shard_keys = jax.random.split(jax.random.fold_in(streams_of[3], 1), REQS * CANDS // CAND_DEV)
    candidate_shard_turns = jax.random.permutation(jax.random.fold_in(streams_of[3], 3), REQS * CANDS // CAND_DEV)
    candidate_shard = jax.vmap(lambda own, number: routed_block(jax.random.fold_in(streams_of[3], 2), own, number, CAND_DEV, N_REQ, 1, CCAP, 2))(candidate_shard_keys, candidate_shard_turns).reshape((REQS, CANDS, 1))
    candidate_row = place_ends(jax.random.randint(streams_of[4], (REQS, CANDS), 0, ROWS_DEV), jax.random.fold_in(streams_of[4], 1), 0, ROWS_DEV - 1).astype(jnp.int32)
    history_length = draw_history_length(jax.random.fold_in(streams_of[11], 71), 0)
    w_query = gaussian(streams_of[6], (D, D), D ** -0.5, 0.375)
    w_key = gaussian(streams_of[7], (D, D), D ** -0.5, 0.375)
    w_value = gaussian(streams_of[8], (D, D), D ** -0.5, 0.375)
    tower_in = gaussian(streams_of[9], (2 * D, TOWER), (2 * D) ** -0.5, 0.25)
    tower_out = gaussian(streams_of[10], (TOWER,), TOWER ** -0.5, 0.1875)
    return {"table": table, "history_shard": history_shard, "history_row": history_row, "candidate_shard": candidate_shard, "candidate_row": candidate_row, "history_length": history_length, "w_query": w_query, "w_key": w_key, "w_value": w_value, "tower_in": tower_in, "tower_out": tower_out}


def reference(table, history_shard, history_row, candidate_shard, candidate_row, history_length, w_query, w_key, w_value, tower_in, tower_out):
    head_size = D // HEADS
    hist_ids = (history_shard[:, :, 0] * ROWS_DEV + history_row).reshape(-1)
    cand_ids = (candidate_shard[:, :, 0] * ROWS_DEV + candidate_row).reshape(-1)
    hist_emb = jnp.take(table, hist_ids, axis=0)
    cand_emb = jnp.take(table, cand_ids, axis=0)
    key_rows = jnp.dot(hist_emb, w_key, preferred_element_type=jnp.float32).astype(jnp.bfloat16)
    value_rows = jnp.dot(hist_emb, w_value, preferred_element_type=jnp.float32).astype(jnp.bfloat16)
    query_row_matrix = jnp.dot(cand_emb, w_query, preferred_element_type=jnp.float32).astype(jnp.bfloat16)
    key_rows = key_rows.reshape(REQS, HIST, HEADS, head_size)
    value_rows = value_rows.reshape(REQS, HIST, HEADS, head_size)
    query_row_matrix = query_row_matrix.reshape(REQS, CANDS // CAND_DEV, CAND_DEV, HEADS, head_size)
    cand_emb = cand_emb.reshape(REQS, CANDS // CAND_DEV, CAND_DEV, D)
    positions = jnp.arange(HIST, dtype=jnp.int32)
    scale_factor = 1.0 / math.sqrt(head_size)

    def one_request(inputs):
        queries, embeds, key_portion_slice, value_portion_slice, length = inputs
        live_mask = positions < length

        def one_block(block_in):
            query_tile_block, embed_block = block_in
            score_matrix = jnp.einsum('zun,aun->zua', query_tile_block.astype(jnp.float32), key_portion_slice.astype(jnp.float32)) * scale_factor
            gate_weights = jnp.where(live_mask[None, None, :], jax.nn.sigmoid(score_matrix), jnp.float32(0.0)).astype(jnp.bfloat16)
            weighted_sum = jnp.einsum('bgo,ogl->bgl', gate_weights.astype(jnp.float32), value_portion_slice.astype(jnp.float32))
            attended = (weighted_sum / jnp.sqrt(length.astype(jnp.float32))).reshape(CAND_DEV, D).astype(jnp.bfloat16)
            pre_act = jnp.dot(embed_block, tower_in[:D], preferred_element_type=jnp.float32) + jnp.dot(attended, tower_in[D:], preferred_element_type=jnp.float32)
            hidden = jax.nn.silu(pre_act).astype(jnp.bfloat16)
            return jnp.dot(hidden, tower_out, preferred_element_type=jnp.float32)
        return lax.map(one_block, (queries, embeds)).reshape(CANDS)
    return lax.map(one_request, (query_row_matrix, cand_emb, key_rows, value_rows, history_length))
```

```python
import math

import jax
import jax.numpy as jnp
from jax import lax
from jax.sharding import PartitionSpec as P

HEADS = 4


def slot_index(shard_ids, n_dest, slot_count, first_slot):
    onehot = (shard_ids[:, None] == jnp.arange(n_dest, dtype=jnp.int32)[None, :]).astype(jnp.int32)
    before = jnp.cumsum(onehot, axis=0) - onehot
    rank = jnp.sum(before * onehot, axis=1)
    return shard_ids * slot_count + first_slot + rank


def body(
    table,
    history_shard,
    history_row,
    candidate_shard,
    candidate_row,
    history_length,
    w_query,
    w_key,
    w_value,
    tower_in,
    tower_out,
):
    n_dest = lax.axis_size("req")
    d_model = table.shape[1]
    hist_shards = history_shard[0, :, 0]
    cand_shards = candidate_shard[0, :, 0]
    hist_dev = hist_shards.shape[0]
    cand_dev = cand_shards.shape[0]
    hist_cap = 4 * hist_dev // n_dest
    cand_cap = 3 * cand_dev // n_dest
    slot_count = hist_cap + cand_cap
    hist_slot = slot_index(hist_shards, n_dest, slot_count, 0)
    cand_slot = slot_index(cand_shards, n_dest, slot_count, hist_cap)
    wanted = jnp.zeros((n_dest * slot_count,), jnp.int32)
    wanted = wanted.at[hist_slot].set(history_row[0]).at[cand_slot].set(candidate_row[0])
    wanted = wanted.reshape(n_dest, slot_count)
    fetched = jnp.take(
        table, lax.all_to_all(wanted, "req", split_axis=0, concat_axis=0, tiled=True), axis=0
    )
    replies = lax.all_to_all(fetched, "req", split_axis=0, concat_axis=0, tiled=True)
    flat_rows = replies.reshape(n_dest * slot_count, d_model)
    hist_emb = jnp.take(flat_rows, hist_slot, axis=0)
    cand_emb = jnp.take(flat_rows, cand_slot, axis=0)
    head_size = d_model // HEADS
    scale_factor = 1.0 / math.sqrt(head_size)
    length = history_length[0]
    w_pair = jnp.concatenate([w_key, w_value], axis=1)
    query_row_matrix = jnp.dot(cand_emb, w_query, preferred_element_type=jnp.float32).astype(
        jnp.bfloat16
    )
    query_row_matrix = query_row_matrix.reshape(cand_dev, HEADS, head_size)
    hist_all = lax.all_gather(hist_emb, "cand", axis=0, tiled=True)
    pair_rows = jnp.dot(hist_all, w_pair, preferred_element_type=jnp.float32).astype(jnp.bfloat16)
    count = pair_rows.shape[0]
    key_portion_slice = pair_rows[:, :d_model].reshape(count, HEADS, head_size)
    value_portion_slice = pair_rows[:, d_model:].reshape(count, HEADS, head_size)
    score_matrix = (
        jnp.einsum(
            "zun,aun->zua", query_row_matrix, key_portion_slice, preferred_element_type=jnp.float32
        )
        * scale_factor
    )
    live_mask = jnp.arange(count, dtype=jnp.int32) < length
    gate_weights = jnp.where(
        live_mask[None, None, :], jax.nn.sigmoid(score_matrix), jnp.float32(0.0)
    ).astype(jnp.bfloat16)
    weighted_sum = jnp.einsum(
        "bgo,ogl->bgl", gate_weights, value_portion_slice, preferred_element_type=jnp.float32
    )
    attended = (
        (weighted_sum / jnp.sqrt(length.astype(jnp.float32)))
        .reshape(cand_dev, d_model)
        .astype(jnp.bfloat16)
    )
    pre_act = jnp.dot(cand_emb, tower_in[:d_model], preferred_element_type=jnp.float32) + jnp.dot(
        attended, tower_in[d_model:], preferred_element_type=jnp.float32
    )
    hidden = jax.nn.silu(pre_act).astype(jnp.bfloat16)
    return jnp.dot(hidden, tower_out, preferred_element_type=jnp.float32)[None, :]


def solution(mesh):
    placed = (
        P("req", None),
        P("req", "cand", None),
        P("req", "cand"),
        P("req", "cand", None),
        P("req", "cand"),
        P("req"),
        P(),
        P(),
        P(),
        P(),
        P(),
    )
    return jax.shard_map(
        body, mesh=mesh, in_specs=placed, out_specs=P("req", "cand"), check_vma=False
    )
```

```python
import math

import jax
import jax.numpy as jnp
from jax import lax
from jax.sharding import PartitionSpec as P

HEADS = 4


def slot_index(shard_ids, n_dest, slot_count, first_slot):
    count = shard_ids.shape[0]
    onehot = (shard_ids[:, None] == jnp.arange(n_dest, dtype=jnp.int32)[None, :]).astype(jnp.bfloat16)
    earlier = lax.broadcasted_iota(jnp.int32, (count, count), 1) < lax.broadcasted_iota(
        jnp.int32, (count, count), 0
    )
    before = jnp.dot(earlier.astype(jnp.bfloat16), onehot, preferred_element_type=jnp.float32)
    rank = jnp.sum(before * onehot.astype(jnp.float32), axis=1).astype(jnp.int32)
    return shard_ids * slot_count + first_slot + rank


def select_rows(slots, n_slots):
    return (slots[:, None] == lax.broadcasted_iota(jnp.int32, (slots.shape[0], n_slots), 1)).astype(
        jnp.bfloat16
    )


def body(
    table,
    history_shard,
    history_row,
    candidate_shard,
    candidate_row,
    history_length,
    w_query,
    w_key,
    w_value,
    tower_in,
    tower_out,
):
    n_dest = lax.axis_size("req")
    d_model = table.shape[1]
    hist_shards = history_shard[0, :, 0]
    cand_shards = candidate_shard[0, :, 0]
    hist_dev = hist_shards.shape[0]
    cand_dev = cand_shards.shape[0]
    hist_cap = 4 * hist_dev // n_dest
    cand_cap = 3 * cand_dev // n_dest
    slot_count = hist_cap + cand_cap
    n_slots = n_dest * slot_count
    hist_slot = slot_index(hist_shards, n_dest, slot_count, 0)
    cand_slot = slot_index(cand_shards, n_dest, slot_count, hist_cap)
    hist_pick = select_rows(hist_slot, n_slots)
    cand_pick = select_rows(cand_slot, n_slots)
    all_pick = jnp.concatenate([hist_pick, cand_pick], axis=0)
    all_rows = jnp.concatenate([history_row[0], candidate_row[0]], axis=0)
    row_parts = jnp.stack([all_rows // 128, all_rows % 128], axis=1).astype(jnp.bfloat16)
    wanted_parts = lax.dot_general(
        all_pick, row_parts, (((0,), (0,)), ((), ())), preferred_element_type=jnp.float32
    ).astype(jnp.int32)
    wanted = (wanted_parts[:, 0] * 128 + wanted_parts[:, 1]).reshape(n_dest, slot_count)
    asked = lax.all_to_all(wanted, "req", split_axis=0, concat_axis=0, tiled=True)
    fetched = jnp.take(table, asked.reshape(-1), axis=0, mode="clip").reshape(
        n_dest, slot_count, d_model
    )
    replies = lax.all_to_all(fetched, "req", split_axis=0, concat_axis=0, tiled=True)
    flat_rows = replies.reshape(n_slots, d_model)
    hist_emb = jnp.dot(hist_pick, flat_rows, preferred_element_type=jnp.float32).astype(jnp.bfloat16)
    cand_emb = jnp.dot(cand_pick, flat_rows, preferred_element_type=jnp.float32).astype(jnp.bfloat16)
    head_size = d_model // HEADS
    scale_factor = 1.0 / math.sqrt(head_size)
    length = history_length[0]
    w_pair = jnp.concatenate([w_key, w_value], axis=1)
    query_row_matrix = jnp.dot(cand_emb, w_query, preferred_element_type=jnp.float32).astype(
        jnp.bfloat16
    )
    query_row_matrix = query_row_matrix.reshape(cand_dev, HEADS, head_size)
    hist_all = lax.all_gather(hist_emb, "cand", axis=0, tiled=True)
    pair_rows = jnp.dot(hist_all, w_pair, preferred_element_type=jnp.float32).astype(jnp.bfloat16)
    count = pair_rows.shape[0]
    key_portion_slice = pair_rows[:, :d_model].reshape(count, HEADS, head_size)
    value_portion_slice = pair_rows[:, d_model:].reshape(count, HEADS, head_size)
    score_matrix = (
        jnp.einsum(
            "zun,aun->zua", query_row_matrix, key_portion_slice, preferred_element_type=jnp.float32
        )
        * scale_factor
    )
    live_mask = jnp.arange(count, dtype=jnp.int32) < length
    gate_weights = jnp.where(
        live_mask[None, None, :], jax.nn.sigmoid(score_matrix), jnp.float32(0.0)
    ).astype(jnp.bfloat16)
    weighted_sum = jnp.einsum(
        "bgo,ogl->bgl", gate_weights, value_portion_slice, preferred_element_type=jnp.float32
    )
    attended = (
        (weighted_sum / jnp.sqrt(length.astype(jnp.float32)))
        .reshape(cand_dev, d_model)
        .astype(jnp.bfloat16)
    )
    pre_act = jnp.dot(cand_emb, tower_in[:d_model], preferred_element_type=jnp.float32) + jnp.dot(
        attended, tower_in[d_model:], preferred_element_type=jnp.float32
    )
    hidden = jax.nn.silu(pre_act).astype(jnp.bfloat16)
    return jnp.dot(hidden, tower_out, preferred_element_type=jnp.float32)[None, :]


def solution(mesh):
    placed = (
        P("req", None),
        P("req", "cand", None),
        P("req", "cand"),
        P("req", "cand", None),
        P("req", "cand"),
        P("req"),
        P(),
        P(),
        P(),
        P(),
        P(),
    )
    return jax.shard_map(
        body, mesh=mesh, in_specs=placed, out_specs=P("req", "cand"), check_vma=False
    )
```

```python
import math

import jax
import jax.numpy as jnp
from jax import lax
from jax.sharding import PartitionSpec as P

HEADS = 4


def slot_index(shard_ids, n_dest, slot_count, first_slot):
    count = shard_ids.shape[0]
    onehot = (shard_ids[:, None] == jnp.arange(n_dest, dtype=jnp.int32)[None, :]).astype(jnp.bfloat16)
    earlier = lax.broadcasted_iota(jnp.int32, (count, count), 1) < lax.broadcasted_iota(
        jnp.int32, (count, count), 0
    )
    before = jnp.dot(earlier.astype(jnp.bfloat16), onehot, preferred_element_type=jnp.float32)
    rank = jnp.sum(before * onehot.astype(jnp.float32), axis=1).astype(jnp.int32)
    return shard_ids * slot_count + first_slot + rank


def select_rows(slots, n_slots):
    return (slots[:, None] == lax.broadcasted_iota(jnp.int32, (slots.shape[0], n_slots), 1)).astype(
        jnp.bfloat16
    )


def wanted_rows(pick, rows):
    row_parts = jnp.stack([rows // 128, rows % 128], axis=1).astype(jnp.bfloat16)
    parts = lax.dot_general(
        pick, row_parts, (((0,), (0,)), ((), ())), preferred_element_type=jnp.float32
    ).astype(jnp.int32)
    return parts[:, 0] * 128 + parts[:, 1]


def body(
    table,
    history_shard,
    history_row,
    candidate_shard,
    candidate_row,
    history_length,
    w_query,
    w_key,
    w_value,
    tower_in,
    tower_out,
):
    n_dest = lax.axis_size("req")
    d_model = table.shape[1]
    hist_shards = history_shard[0, :, 0]
    cand_shards = candidate_shard[0, :, 0]
    hist_dev = hist_shards.shape[0]
    cand_dev = cand_shards.shape[0]
    hist_cap = 4 * hist_dev // n_dest
    cand_cap = 3 * cand_dev // n_dest
    hist_slot = slot_index(hist_shards, n_dest, hist_cap, 0)
    cand_slot = slot_index(cand_shards, n_dest, cand_cap, 0)
    hist_pick = select_rows(hist_slot, n_dest * hist_cap)
    cand_pick = select_rows(cand_slot, n_dest * cand_cap)
    hist_wanted = wanted_rows(hist_pick, history_row[0]).reshape(n_dest, hist_cap)
    cand_wanted = wanted_rows(cand_pick, candidate_row[0]).reshape(n_dest, cand_cap)
    asked = lax.all_to_all(
        jnp.concatenate([hist_wanted, cand_wanted], axis=1),
        "req",
        split_axis=0,
        concat_axis=0,
        tiled=True,
    )
    hist_fetched = jnp.take(table, asked[:, :hist_cap].reshape(-1), axis=0, mode="clip")
    hist_replies = lax.all_to_all(
        hist_fetched.reshape(n_dest, hist_cap, d_model), "req", split_axis=0, concat_axis=0, tiled=True
    ).reshape(n_dest * hist_cap, d_model)
    cand_fetched = jnp.take(table, asked[:, hist_cap:].reshape(-1), axis=0, mode="clip")
    cand_replies = lax.all_to_all(
        cand_fetched.reshape(n_dest, cand_cap, d_model), "req", split_axis=0, concat_axis=0, tiled=True
    ).reshape(n_dest * cand_cap, d_model)
    hist_emb = jnp.dot(hist_pick, hist_replies, preferred_element_type=jnp.float32).astype(jnp.bfloat16)
    cand_emb = jnp.dot(cand_pick, cand_replies, preferred_element_type=jnp.float32).astype(jnp.bfloat16)
    head_size = d_model // HEADS
    scale_factor = 1.0 / math.sqrt(head_size)
    length = history_length[0]
    w_pair = jnp.concatenate([w_key, w_value], axis=1)
    query_row_matrix = jnp.dot(cand_emb, w_query, preferred_element_type=jnp.float32).astype(
        jnp.bfloat16
    )
    query_row_matrix = query_row_matrix.reshape(cand_dev, HEADS, head_size)
    hist_all = lax.all_gather(hist_emb, "cand", axis=0, tiled=True)
    pair_rows = jnp.dot(hist_all, w_pair, preferred_element_type=jnp.float32).astype(jnp.bfloat16)
    count = pair_rows.shape[0]
    key_portion_slice = pair_rows[:, :d_model].reshape(count, HEADS, head_size)
    value_portion_slice = pair_rows[:, d_model:].reshape(count, HEADS, head_size)
    score_matrix = (
        jnp.einsum(
            "zun,aun->zua", query_row_matrix, key_portion_slice, preferred_element_type=jnp.float32
        )
        * scale_factor
    )
    live_mask = jnp.arange(count, dtype=jnp.int32) < length
    gate_weights = jnp.where(
        live_mask[None, None, :], jax.nn.sigmoid(score_matrix), jnp.float32(0.0)
    ).astype(jnp.bfloat16)
    weighted_sum = jnp.einsum(
        "bgo,ogl->bgl", gate_weights, value_portion_slice, preferred_element_type=jnp.float32
    )
    attended = (
        (weighted_sum / jnp.sqrt(length.astype(jnp.float32)))
        .reshape(cand_dev, d_model)
        .astype(jnp.bfloat16)
    )
    pre_act = jnp.dot(cand_emb, tower_in[:d_model], preferred_element_type=jnp.float32) + jnp.dot(
        attended, tower_in[d_model:], preferred_element_type=jnp.float32
    )
    hidden = jax.nn.silu(pre_act).astype(jnp.bfloat16)
    return jnp.dot(hidden, tower_out, preferred_element_type=jnp.float32)[None, :]


def solution(mesh):
    placed = (
        P("req", None),
        P("req", "cand", None),
        P("req", "cand"),
        P("req", "cand", None),
        P("req", "cand"),
        P("req"),
        P(),
        P(),
        P(),
        P(),
        P(),
    )
    return jax.shard_map(
        body, mesh=mesh, in_specs=placed, out_specs=P("req", "cand"), check_vma=False
    )
```

```python
import math

import jax
import jax.numpy as jnp
from jax import lax
from jax.experimental import pallas as pl
from jax.experimental.pallas import tpu as pltpu
from jax.sharding import PartitionSpec as P

HEADS = 4


def slot_index(shard_ids, n_dest, slot_count, first_slot):
    count = shard_ids.shape[0]
    onehot = (shard_ids[:, None] == jnp.arange(n_dest, dtype=jnp.int32)[None, :]).astype(jnp.bfloat16)
    earlier = lax.broadcasted_iota(jnp.int32, (count, count), 1) < lax.broadcasted_iota(
        jnp.int32, (count, count), 0
    )
    before = jnp.dot(earlier.astype(jnp.bfloat16), onehot, preferred_element_type=jnp.float32)
    rank = jnp.sum(before * onehot.astype(jnp.float32), axis=1).astype(jnp.int32)
    return shard_ids * slot_count + first_slot + rank


def select_rows(slots, n_slots):
    return (slots[:, None] == lax.broadcasted_iota(jnp.int32, (slots.shape[0], n_slots), 1)).astype(
        jnp.bfloat16
    )


def gather_kernel(idx_ref, table_ref, out_ref, sem):
    count = out_ref.shape[0] // 2

    def issue(i, carry):
        first = pl.multiple_of(idx_ref[i] // 2 * 2, 2)
        pltpu.make_async_copy(
            table_ref.at[pl.ds(first, 2)], out_ref.at[pl.ds(pl.multiple_of(2 * i, 2), 2)], sem
        ).start()
        return carry

    lax.fori_loop(0, count, issue, 0, unroll=8)
    pltpu.make_async_copy(table_ref.at[pl.ds(0, 2 * count)], out_ref, sem).wait()


def gather_rows(table, idx):
    count, width = idx.shape[0], table.shape[1]
    pairs = pl.pallas_call(
        gather_kernel,
        out_shape=jax.ShapeDtypeStruct((2 * count, width), table.dtype),
        grid_spec=pltpu.PrefetchScalarGridSpec(
            num_scalar_prefetch=1,
            grid=(1,),
            in_specs=[pl.BlockSpec(memory_space=pl.ANY)],
            out_specs=pl.BlockSpec((2 * count, width), lambda i, idx_ref: (0, 0)),
            scratch_shapes=[pltpu.SemaphoreType.DMA(())],
        ),
        cost_estimate=pl.CostEstimate(
            flops=0, transcendentals=0, bytes_accessed=4 * count * width * table.dtype.itemsize
        ),
    )(idx, table).reshape(count, 2, width)
    return jnp.where((idx % 2 == 1)[:, None], pairs[:, 1], pairs[:, 0])


def body(
    table,
    history_shard,
    history_row,
    candidate_shard,
    candidate_row,
    history_length,
    w_query,
    w_key,
    w_value,
    tower_in,
    tower_out,
):
    n_dest = lax.axis_size("req")
    d_model = table.shape[1]
    hist_shards = history_shard[0, :, 0]
    cand_shards = candidate_shard[0, :, 0]
    hist_dev = hist_shards.shape[0]
    cand_dev = cand_shards.shape[0]
    hist_cap = 4 * hist_dev // n_dest
    cand_cap = 3 * cand_dev // n_dest
    slot_count = hist_cap + cand_cap
    n_slots = n_dest * slot_count
    hist_slot = slot_index(hist_shards, n_dest, slot_count, 0)
    cand_slot = slot_index(cand_shards, n_dest, slot_count, hist_cap)
    hist_pick = select_rows(hist_slot, n_slots)
    cand_pick = select_rows(cand_slot, n_slots)
    all_pick = jnp.concatenate([hist_pick, cand_pick], axis=0)
    all_rows = jnp.concatenate([history_row[0], candidate_row[0]], axis=0)
    row_parts = jnp.stack([all_rows // 128, all_rows % 128], axis=1).astype(jnp.bfloat16)
    wanted_parts = lax.dot_general(
        all_pick, row_parts, (((0,), (0,)), ((), ())), preferred_element_type=jnp.float32
    ).astype(jnp.int32)
    wanted = (wanted_parts[:, 0] * 128 + wanted_parts[:, 1]).reshape(n_dest, slot_count)
    asked = lax.all_to_all(wanted, "req", split_axis=0, concat_axis=0, tiled=True)
    fetched = gather_rows(table, jnp.clip(asked.reshape(-1), 0, table.shape[0] - 1)).reshape(
        n_dest, slot_count, d_model
    )
    replies = lax.all_to_all(fetched, "req", split_axis=0, concat_axis=0, tiled=True)
    flat_rows = replies.reshape(n_slots, d_model)
    hist_emb = jnp.dot(hist_pick, flat_rows, preferred_element_type=jnp.float32).astype(jnp.bfloat16)
    cand_emb = jnp.dot(cand_pick, flat_rows, preferred_element_type=jnp.float32).astype(jnp.bfloat16)
    head_size = d_model // HEADS
    scale_factor = 1.0 / math.sqrt(head_size)
    length = history_length[0]
    w_pair = jnp.concatenate([w_key, w_value], axis=1)
    query_row_matrix = jnp.dot(cand_emb, w_query, preferred_element_type=jnp.float32).astype(
        jnp.bfloat16
    )
    query_row_matrix = query_row_matrix.reshape(cand_dev, HEADS, head_size)
    hist_all = lax.all_gather(hist_emb, "cand", axis=0, tiled=True)
    pair_rows = jnp.dot(hist_all, w_pair, preferred_element_type=jnp.float32).astype(jnp.bfloat16)
    count = pair_rows.shape[0]
    key_portion_slice = pair_rows[:, :d_model].reshape(count, HEADS, head_size)
    value_portion_slice = pair_rows[:, d_model:].reshape(count, HEADS, head_size)
    score_matrix = (
        jnp.einsum(
            "zun,aun->zua", query_row_matrix, key_portion_slice, preferred_element_type=jnp.float32
        )
        * scale_factor
    )
    live_mask = jnp.arange(count, dtype=jnp.int32) < length
    gate_weights = jnp.where(
        live_mask[None, None, :], jax.nn.sigmoid(score_matrix), jnp.float32(0.0)
    ).astype(jnp.bfloat16)
    weighted_sum = jnp.einsum(
        "bgo,ogl->bgl", gate_weights, value_portion_slice, preferred_element_type=jnp.float32
    )
    attended = (
        (weighted_sum / jnp.sqrt(length.astype(jnp.float32)))
        .reshape(cand_dev, d_model)
        .astype(jnp.bfloat16)
    )
    pre_act = jnp.dot(cand_emb, tower_in[:d_model], preferred_element_type=jnp.float32) + jnp.dot(
        attended, tower_in[d_model:], preferred_element_type=jnp.float32
    )
    hidden = jax.nn.silu(pre_act).astype(jnp.bfloat16)
    return jnp.dot(hidden, tower_out, preferred_element_type=jnp.float32)[None, :]


def solution(mesh):
    placed = (
        P("req", None),
        P("req", "cand", None),
        P("req", "cand"),
        P("req", "cand", None),
        P("req", "cand"),
        P("req"),
        P(),
        P(),
        P(),
        P(),
        P(),
    )
    return jax.shard_map(
        body, mesh=mesh, in_specs=placed, out_specs=P("req", "cand"), check_vma=False
    )
```

```python
import math

import jax
import jax.numpy as jnp
from jax import lax
from jax.sharding import PartitionSpec as P

HEADS = 4


def slot_index(shard_ids, n_dest, slot_count, first_slot):
    count = shard_ids.shape[0]
    onehot = (shard_ids[:, None] == jnp.arange(n_dest, dtype=jnp.int32)[None, :]).astype(jnp.bfloat16)
    earlier = lax.broadcasted_iota(jnp.int32, (count, count), 1) < lax.broadcasted_iota(
        jnp.int32, (count, count), 0
    )
    before = jnp.dot(earlier.astype(jnp.bfloat16), onehot, preferred_element_type=jnp.float32)
    rank = jnp.sum(before * onehot.astype(jnp.float32), axis=1).astype(jnp.int32)
    return shard_ids * slot_count + first_slot + rank


def select_rows(slots, n_slots):
    return (slots[:, None] == lax.broadcasted_iota(jnp.int32, (slots.shape[0], n_slots), 1)).astype(
        jnp.bfloat16
    )


def gather_over_cand(rows):
    n_cand = lax.axis_size("cand")
    me = lax.axis_index("cand")
    blocks, sources = [rows], [me]
    for hop in range(2, n_cand, 2):
        blocks.append(lax.ppermute(rows, "cand", [(i, (i + hop) % n_cand) for i in range(n_cand)]))
        sources.append((me - hop) % n_cand)
    mine = jnp.stack(blocks, axis=0)
    partner = lax.ppermute(mine, "cand", [(i, i ^ 1) for i in range(n_cand)])
    held = jnp.concatenate([mine, partner], axis=0)
    source = jnp.stack(sources)
    source = jnp.concatenate([source, source ^ 1])
    order = jnp.argmax(source[None, :] == jnp.arange(n_cand)[:, None], axis=1)
    return jnp.take(held, order, axis=0).reshape(-1, rows.shape[1])


def body(
    table,
    history_shard,
    history_row,
    candidate_shard,
    candidate_row,
    history_length,
    w_query,
    w_key,
    w_value,
    tower_in,
    tower_out,
):
    n_dest = lax.axis_size("req")
    d_model = table.shape[1]
    hist_shards = history_shard[0, :, 0]
    cand_shards = candidate_shard[0, :, 0]
    hist_dev = hist_shards.shape[0]
    cand_dev = cand_shards.shape[0]
    hist_cap = 4 * hist_dev // n_dest
    cand_cap = 3 * cand_dev // n_dest
    slot_count = hist_cap + cand_cap
    n_slots = n_dest * slot_count
    hist_slot = slot_index(hist_shards, n_dest, slot_count, 0)
    cand_slot = slot_index(cand_shards, n_dest, slot_count, hist_cap)
    hist_pick = select_rows(hist_slot, n_slots)
    cand_pick = select_rows(cand_slot, n_slots)
    all_pick = jnp.concatenate([hist_pick, cand_pick], axis=0)
    all_rows = jnp.concatenate([history_row[0], candidate_row[0]], axis=0)
    row_parts = jnp.stack([all_rows // 128, all_rows % 128], axis=1).astype(jnp.bfloat16)
    wanted_parts = lax.dot_general(
        all_pick, row_parts, (((0,), (0,)), ((), ())), preferred_element_type=jnp.float32
    ).astype(jnp.int32)
    wanted = (wanted_parts[:, 0] * 128 + wanted_parts[:, 1]).reshape(n_dest, slot_count)
    asked = lax.all_to_all(wanted, "req", split_axis=0, concat_axis=0, tiled=True)
    fetched = jnp.take(table, asked.reshape(-1), axis=0, mode="clip").reshape(
        n_dest, slot_count, d_model
    )
    replies = lax.all_to_all(fetched, "req", split_axis=0, concat_axis=0, tiled=True)
    flat_rows = replies.reshape(n_slots, d_model)
    hist_emb = jnp.dot(hist_pick, flat_rows, preferred_element_type=jnp.float32).astype(jnp.bfloat16)
    cand_emb = jnp.dot(cand_pick, flat_rows, preferred_element_type=jnp.float32).astype(jnp.bfloat16)
    head_size = d_model // HEADS
    scale_factor = 1.0 / math.sqrt(head_size)
    length = history_length[0]
    w_pair = jnp.concatenate([w_key, w_value], axis=1)
    query_row_matrix = jnp.dot(cand_emb, w_query, preferred_element_type=jnp.float32).astype(
        jnp.bfloat16
    )
    query_row_matrix = query_row_matrix.reshape(cand_dev, HEADS, head_size)
    hist_all = gather_over_cand(hist_emb)
    pair_rows = jnp.dot(hist_all, w_pair, preferred_element_type=jnp.float32).astype(jnp.bfloat16)
    count = pair_rows.shape[0]
    key_portion_slice = pair_rows[:, :d_model].reshape(count, HEADS, head_size)
    value_portion_slice = pair_rows[:, d_model:].reshape(count, HEADS, head_size)
    score_matrix = (
        jnp.einsum(
            "zun,aun->zua", query_row_matrix, key_portion_slice, preferred_element_type=jnp.float32
        )
        * scale_factor
    )
    live_mask = jnp.arange(count, dtype=jnp.int32) < length
    gate_weights = jnp.where(
        live_mask[None, None, :], jax.nn.sigmoid(score_matrix), jnp.float32(0.0)
    ).astype(jnp.bfloat16)
    weighted_sum = jnp.einsum(
        "bgo,ogl->bgl", gate_weights, value_portion_slice, preferred_element_type=jnp.float32
    )
    attended = (
        (weighted_sum / jnp.sqrt(length.astype(jnp.float32)))
        .reshape(cand_dev, d_model)
        .astype(jnp.bfloat16)
    )
    pre_act = jnp.dot(cand_emb, tower_in[:d_model], preferred_element_type=jnp.float32) + jnp.dot(
        attended, tower_in[d_model:], preferred_element_type=jnp.float32
    )
    hidden = jax.nn.silu(pre_act).astype(jnp.bfloat16)
    return jnp.dot(hidden, tower_out, preferred_element_type=jnp.float32)[None, :]


def solution(mesh):
    placed = (
        P("req", None),
        P("req", "cand", None),
        P("req", "cand"),
        P("req", "cand", None),
        P("req", "cand"),
        P("req"),
        P(),
        P(),
        P(),
        P(),
        P(),
    )
    return jax.shard_map(
        body, mesh=mesh, in_specs=placed, out_specs=P("req", "cand"), check_vma=False
    )
```

```python
import math

import jax
import jax.numpy as jnp
from jax import lax
from jax.sharding import PartitionSpec as P

HEADS = 4


def slot_index(shard_ids, n_dest, slot_count, first_slot):
    count = shard_ids.shape[0]
    onehot = (shard_ids[:, None] == jnp.arange(n_dest, dtype=jnp.int32)[None, :]).astype(jnp.bfloat16)
    earlier = lax.broadcasted_iota(jnp.int32, (count, count), 1) < lax.broadcasted_iota(
        jnp.int32, (count, count), 0
    )
    before = jnp.dot(earlier.astype(jnp.bfloat16), onehot, preferred_element_type=jnp.float32)
    rank = jnp.sum(before * onehot.astype(jnp.float32), axis=1).astype(jnp.int32)
    return shard_ids * slot_count + first_slot + rank


def select_rows(slots, n_slots):
    return (slots[:, None] == lax.broadcasted_iota(jnp.int32, (slots.shape[0], n_slots), 1)).astype(
        jnp.bfloat16
    )


def gather_over_cand(rows):
    n_cand = lax.axis_size("cand")
    me = lax.axis_index("cand")
    blocks, sources = [rows], [me]
    for hop in range(2, n_cand, 2):
        blocks.append(lax.ppermute(rows, "cand", [(i, (i + hop) % n_cand) for i in range(n_cand)]))
        sources.append((me - hop) % n_cand)
    mine = jnp.stack(blocks, axis=0)
    partner = lax.ppermute(mine, "cand", [(i, i ^ 1) for i in range(n_cand)])
    held = jnp.concatenate([mine, partner], axis=0)
    source = jnp.stack(sources)
    source = jnp.concatenate([source, source ^ 1])
    order = jnp.argmax(source[None, :] == jnp.arange(n_cand)[:, None], axis=1)
    return jnp.take(held, order, axis=0).reshape(-1, rows.shape[1])


def swap_over_req(blocks):
    n_req = blocks.shape[0]
    swapped = [blocks[0]]
    for hop in range(1, n_req):
        swapped.append(lax.ppermute(blocks[hop], "req", [(i, i ^ hop) for i in range(n_req)]))
    return jnp.stack(swapped, axis=0)


def body(
    table,
    history_shard,
    history_row,
    candidate_shard,
    candidate_row,
    history_length,
    w_query,
    w_key,
    w_value,
    tower_in,
    tower_out,
):
    n_dest = lax.axis_size("req")
    d_model = table.shape[1]
    hist_shards = history_shard[0, :, 0]
    cand_shards = candidate_shard[0, :, 0]
    hist_dev = hist_shards.shape[0]
    cand_dev = cand_shards.shape[0]
    hist_cap = 4 * hist_dev // n_dest
    cand_cap = 3 * cand_dev // n_dest
    slot_count = hist_cap + cand_cap
    n_slots = n_dest * slot_count
    assert n_dest & (n_dest - 1) == 0
    me = lax.axis_index("req")
    hist_slot = slot_index(hist_shards ^ me, n_dest, slot_count, 0)
    cand_slot = slot_index(cand_shards ^ me, n_dest, slot_count, hist_cap)
    hist_pick = select_rows(hist_slot, n_slots)
    cand_pick = select_rows(cand_slot, n_slots)
    all_pick = jnp.concatenate([hist_pick, cand_pick], axis=0)
    all_rows = jnp.concatenate([history_row[0], candidate_row[0]], axis=0)
    row_parts = jnp.stack([all_rows // 128, all_rows % 128], axis=1).astype(jnp.bfloat16)
    wanted_parts = lax.dot_general(
        all_pick, row_parts, (((0,), (0,)), ((), ())), preferred_element_type=jnp.float32
    ).astype(jnp.int32)
    wanted = (wanted_parts[:, 0] * 128 + wanted_parts[:, 1]).reshape(n_dest, slot_count)
    asked = swap_over_req(wanted)
    fetched = jnp.take(table, asked.reshape(-1), axis=0, mode="clip").reshape(
        n_dest, slot_count, d_model
    )
    replies = swap_over_req(fetched)
    flat_rows = replies.reshape(n_slots, d_model)
    hist_emb = jnp.dot(hist_pick, flat_rows, preferred_element_type=jnp.float32).astype(jnp.bfloat16)
    cand_emb = jnp.dot(cand_pick, flat_rows, preferred_element_type=jnp.float32).astype(jnp.bfloat16)
    head_size = d_model // HEADS
    scale_factor = 1.0 / math.sqrt(head_size)
    length = history_length[0]
    w_pair = jnp.concatenate([w_key, w_value], axis=1)
    query_row_matrix = jnp.dot(cand_emb, w_query, preferred_element_type=jnp.float32).astype(
        jnp.bfloat16
    )
    query_row_matrix = query_row_matrix.reshape(cand_dev, HEADS, head_size)
    hist_all = gather_over_cand(hist_emb)
    pair_rows = jnp.dot(hist_all, w_pair, preferred_element_type=jnp.float32).astype(jnp.bfloat16)
    count = pair_rows.shape[0]
    key_portion_slice = pair_rows[:, :d_model].reshape(count, HEADS, head_size)
    value_portion_slice = pair_rows[:, d_model:].reshape(count, HEADS, head_size)
    score_matrix = (
        jnp.einsum(
            "zun,aun->zua", query_row_matrix, key_portion_slice, preferred_element_type=jnp.float32
        )
        * scale_factor
    )
    live_mask = jnp.arange(count, dtype=jnp.int32) < length
    gate_weights = jnp.where(
        live_mask[None, None, :], jax.nn.sigmoid(score_matrix), jnp.float32(0.0)
    ).astype(jnp.bfloat16)
    weighted_sum = jnp.einsum(
        "bgo,ogl->bgl", gate_weights, value_portion_slice, preferred_element_type=jnp.float32
    )
    attended = (
        (weighted_sum / jnp.sqrt(length.astype(jnp.float32)))
        .reshape(cand_dev, d_model)
        .astype(jnp.bfloat16)
    )
    pre_act = jnp.dot(cand_emb, tower_in[:d_model], preferred_element_type=jnp.float32) + jnp.dot(
        attended, tower_in[d_model:], preferred_element_type=jnp.float32
    )
    hidden = jax.nn.silu(pre_act).astype(jnp.bfloat16)
    return jnp.dot(hidden, tower_out, preferred_element_type=jnp.float32)[None, :]


def solution(mesh):
    placed = (
        P("req", None),
        P("req", "cand", None),
        P("req", "cand"),
        P("req", "cand", None),
        P("req", "cand"),
        P("req"),
        P(),
        P(),
        P(),
        P(),
        P(),
    )
    return jax.shard_map(
        body, mesh=mesh, in_specs=placed, out_specs=P("req", "cand"), check_vma=False
    )
```

```python
import math

import jax
import jax.numpy as jnp
from jax import lax
from jax.sharding import PartitionSpec as P

HEADS = 4


def slot_index(shard_ids, n_dest, slot_count, first_slot):
    count = shard_ids.shape[0]
    onehot = (shard_ids[:, None] == jnp.arange(n_dest, dtype=jnp.int32)[None, :]).astype(jnp.bfloat16)
    earlier = lax.broadcasted_iota(jnp.int32, (count, count), 1) < lax.broadcasted_iota(
        jnp.int32, (count, count), 0
    )
    before = jnp.dot(earlier.astype(jnp.bfloat16), onehot, preferred_element_type=jnp.float32)
    rank = jnp.sum(before * onehot.astype(jnp.float32), axis=1).astype(jnp.int32)
    return shard_ids * slot_count + first_slot + rank


def select_rows(slots, n_slots):
    return (slots[:, None] == lax.broadcasted_iota(jnp.int32, (slots.shape[0], n_slots), 1)).astype(
        jnp.bfloat16
    )


def gather_over_cand(rows):
    n_cand = lax.axis_size("cand")
    me = lax.axis_index("cand")
    blocks, sources = [rows], [me]
    for hop in range(2, n_cand, 2):
        blocks.append(lax.ppermute(rows, "cand", [(i, (i + hop) % n_cand) for i in range(n_cand)]))
        sources.append((me - hop) % n_cand)
    mine = jnp.stack(blocks, axis=0)
    partner = lax.ppermute(mine, "cand", [(i, i ^ 1) for i in range(n_cand)])
    held = jnp.concatenate([mine, partner], axis=0)
    source = jnp.stack(sources)
    source = jnp.concatenate([source, source ^ 1])
    order = jnp.argmax(source[None, :] == jnp.arange(n_cand)[:, None], axis=1)
    return jnp.take(held, order, axis=0).reshape(-1, rows.shape[1])


def wanted_rows(pick, rows):
    row_parts = jnp.stack([rows // 128, rows % 128], axis=1).astype(jnp.bfloat16)
    parts = lax.dot_general(
        pick, row_parts, (((0,), (0,)), ((), ())), preferred_element_type=jnp.float32
    ).astype(jnp.int32)
    return parts[:, 0] * 128 + parts[:, 1]


def swap_over_req(blocks):
    n_req = blocks.shape[0]
    swapped = [blocks[0]]
    for hop in range(1, n_req):
        swapped.append(lax.ppermute(blocks[hop], "req", [(i, i ^ hop) for i in range(n_req)]))
    return jnp.stack(swapped, axis=0)


def body(
    table,
    history_shard,
    history_row,
    candidate_shard,
    candidate_row,
    history_length,
    w_query,
    w_key,
    w_value,
    tower_in,
    tower_out,
):
    n_dest = lax.axis_size("req")
    d_model = table.shape[1]
    hist_shards = history_shard[0, :, 0]
    cand_shards = candidate_shard[0, :, 0]
    hist_dev = hist_shards.shape[0]
    cand_dev = cand_shards.shape[0]
    hist_cap = 4 * hist_dev // n_dest
    cand_cap = 3 * cand_dev // n_dest
    assert n_dest & (n_dest - 1) == 0
    me = lax.axis_index("req")
    hist_slot = slot_index(hist_shards ^ me, n_dest, hist_cap, 0)
    cand_slot = slot_index(cand_shards ^ me, n_dest, cand_cap, 0)
    hist_pick = select_rows(hist_slot, n_dest * hist_cap)
    cand_pick = select_rows(cand_slot, n_dest * cand_cap)
    hist_wanted = wanted_rows(hist_pick, history_row[0]).reshape(n_dest, hist_cap)
    cand_wanted = wanted_rows(cand_pick, candidate_row[0]).reshape(n_dest, cand_cap)
    asked = swap_over_req(jnp.concatenate([hist_wanted, cand_wanted], axis=1))
    fetched = jnp.take(table, asked.reshape(-1), axis=0, mode="clip").reshape(
        n_dest, hist_cap + cand_cap, d_model
    )
    hist_replies = swap_over_req(fetched[:, :hist_cap]).reshape(n_dest * hist_cap, d_model)
    cand_replies = swap_over_req(fetched[:, hist_cap:]).reshape(n_dest * cand_cap, d_model)
    hist_emb = jnp.dot(hist_pick, hist_replies, preferred_element_type=jnp.float32).astype(jnp.bfloat16)
    cand_emb = jnp.dot(cand_pick, cand_replies, preferred_element_type=jnp.float32).astype(jnp.bfloat16)
    head_size = d_model // HEADS
    scale_factor = 1.0 / math.sqrt(head_size)
    length = history_length[0]
    w_pair = jnp.concatenate([w_key, w_value], axis=1)
    query_row_matrix = jnp.dot(cand_emb, w_query, preferred_element_type=jnp.float32).astype(
        jnp.bfloat16
    )
    query_row_matrix = query_row_matrix.reshape(cand_dev, HEADS, head_size)
    hist_all = gather_over_cand(hist_emb)
    pair_rows = jnp.dot(hist_all, w_pair, preferred_element_type=jnp.float32).astype(jnp.bfloat16)
    count = pair_rows.shape[0]
    key_portion_slice = pair_rows[:, :d_model].reshape(count, HEADS, head_size)
    value_portion_slice = pair_rows[:, d_model:].reshape(count, HEADS, head_size)
    score_matrix = (
        jnp.einsum(
            "zun,aun->zua", query_row_matrix, key_portion_slice, preferred_element_type=jnp.float32
        )
        * scale_factor
    )
    live_mask = jnp.arange(count, dtype=jnp.int32) < length
    gate_weights = jnp.where(
        live_mask[None, None, :], jax.nn.sigmoid(score_matrix), jnp.float32(0.0)
    ).astype(jnp.bfloat16)
    weighted_sum = jnp.einsum(
        "bgo,ogl->bgl", gate_weights, value_portion_slice, preferred_element_type=jnp.float32
    )
    attended = (
        (weighted_sum / jnp.sqrt(length.astype(jnp.float32)))
        .reshape(cand_dev, d_model)
        .astype(jnp.bfloat16)
    )
    pre_act = jnp.dot(cand_emb, tower_in[:d_model], preferred_element_type=jnp.float32) + jnp.dot(
        attended, tower_in[d_model:], preferred_element_type=jnp.float32
    )
    hidden = jax.nn.silu(pre_act).astype(jnp.bfloat16)
    return jnp.dot(hidden, tower_out, preferred_element_type=jnp.float32)[None, :]


def solution(mesh):
    placed = (
        P("req", None),
        P("req", "cand", None),
        P("req", "cand"),
        P("req", "cand", None),
        P("req", "cand"),
        P("req"),
        P(),
        P(),
        P(),
        P(),
        P(),
    )
    return jax.shard_map(
        body, mesh=mesh, in_specs=placed, out_specs=P("req", "cand"), check_vma=False
    )
```

```python
import math

import jax
import jax.numpy as jnp
from jax import lax
from jax.sharding import PartitionSpec as P

HEADS = 4


def slot_index(shard_ids, slot_count):
    count = shard_ids.shape[0]
    earlier = lax.broadcasted_iota(jnp.int32, (count, count), 1) < lax.broadcasted_iota(
        jnp.int32, (count, count), 0
    )
    same = (shard_ids[:, None] == shard_ids[None, :]) & earlier
    rank = jnp.sum(same.astype(jnp.int32), axis=1)
    return shard_ids * slot_count + rank


def select_rows(slots, n_slots):
    return (slots[:, None] == lax.broadcasted_iota(jnp.int32, (slots.shape[0], n_slots), 1)).astype(
        jnp.bfloat16
    )


def gather_over_cand(rows):
    n_cand = lax.axis_size("cand")
    me = lax.axis_index("cand")
    blocks, sources = [rows], [me]
    for hop in range(2, n_cand, 2):
        blocks.append(lax.ppermute(rows, "cand", [(i, (i + hop) % n_cand) for i in range(n_cand)]))
        sources.append((me - hop) % n_cand)
    mine = jnp.stack(blocks, axis=0)
    partner = lax.ppermute(mine, "cand", [(i, i ^ 1) for i in range(n_cand)])
    held = jnp.concatenate([mine, partner], axis=0)
    source = jnp.stack(sources)
    source = jnp.concatenate([source, source ^ 1])
    order = jnp.argmax(source[None, :] == jnp.arange(n_cand)[:, None], axis=1)
    return jnp.take(held, order, axis=0).reshape(-1, rows.shape[1])


def wanted_rows(slots, n_slots, rows):
    pick_t = (lax.broadcasted_iota(jnp.int32, (n_slots, slots.shape[0]), 0) == slots[None, :]).astype(
        jnp.bfloat16
    )
    row_parts = jnp.stack([rows // 128, rows % 128], axis=1).astype(jnp.bfloat16)
    parts = jnp.dot(pick_t, row_parts, preferred_element_type=jnp.float32).astype(jnp.int32)
    return parts[:, 0] * 128 + parts[:, 1]


def swap_over_req(blocks):
    n_req = blocks.shape[0]
    swapped = [blocks[0]]
    for hop in range(1, n_req):
        swapped.append(lax.ppermute(blocks[hop], "req", [(i, i ^ hop) for i in range(n_req)]))
    return jnp.stack(swapped, axis=0)


def body(
    table,
    history_shard,
    history_row,
    candidate_shard,
    candidate_row,
    history_length,
    w_query,
    w_key,
    w_value,
    tower_in,
    tower_out,
):
    n_dest = lax.axis_size("req")
    d_model = table.shape[1]
    hist_shards = history_shard[0, :, 0]
    cand_shards = candidate_shard[0, :, 0]
    hist_dev = hist_shards.shape[0]
    cand_dev = cand_shards.shape[0]
    hist_cap = 4 * hist_dev // n_dest
    cand_cap = 3 * cand_dev // n_dest
    assert n_dest & (n_dest - 1) == 0
    me = lax.axis_index("req")
    hist_slot = slot_index(hist_shards ^ me, hist_cap)
    cand_slot = slot_index(cand_shards ^ me, cand_cap)
    hist_pick = select_rows(hist_slot, n_dest * hist_cap)
    cand_pick = select_rows(cand_slot, n_dest * cand_cap)
    hist_wanted = wanted_rows(hist_slot, n_dest * hist_cap, history_row[0]).reshape(n_dest, hist_cap)
    cand_wanted = wanted_rows(cand_slot, n_dest * cand_cap, candidate_row[0]).reshape(n_dest, cand_cap)
    asked = swap_over_req(jnp.concatenate([hist_wanted, cand_wanted], axis=1))
    fetched = jnp.take(table, asked.reshape(-1), axis=0, mode="clip").reshape(
        n_dest, hist_cap + cand_cap, d_model
    )
    hist_replies = swap_over_req(fetched[:, :hist_cap]).reshape(n_dest * hist_cap, d_model)
    cand_replies = swap_over_req(fetched[:, hist_cap:]).reshape(n_dest * cand_cap, d_model)
    hist_emb = jnp.dot(hist_pick, hist_replies, preferred_element_type=jnp.float32).astype(jnp.bfloat16)
    cand_emb = jnp.dot(cand_pick, cand_replies, preferred_element_type=jnp.float32).astype(jnp.bfloat16)
    head_size = d_model // HEADS
    scale_factor = 1.0 / math.sqrt(head_size)
    length = history_length[0]
    w_pair = jnp.concatenate([w_key, w_value], axis=1)
    query_row_matrix = jnp.dot(cand_emb, w_query, preferred_element_type=jnp.float32).astype(
        jnp.bfloat16
    )
    query_row_matrix = query_row_matrix.reshape(cand_dev, HEADS, head_size)
    hist_all = gather_over_cand(hist_emb)
    pair_rows = jnp.dot(hist_all, w_pair, preferred_element_type=jnp.float32).astype(jnp.bfloat16)
    count = pair_rows.shape[0]
    key_portion_slice = pair_rows[:, :d_model].reshape(count, HEADS, head_size)
    value_portion_slice = pair_rows[:, d_model:].reshape(count, HEADS, head_size)
    score_matrix = (
        jnp.einsum(
            "zun,aun->zua", query_row_matrix, key_portion_slice, preferred_element_type=jnp.float32
        )
        * scale_factor
    )
    live_mask = jnp.arange(count, dtype=jnp.int32) < length
    gate_weights = jnp.where(
        live_mask[None, None, :], jax.nn.sigmoid(score_matrix), jnp.float32(0.0)
    ).astype(jnp.bfloat16)
    weighted_sum = jnp.einsum(
        "bgo,ogl->bgl", gate_weights, value_portion_slice, preferred_element_type=jnp.float32
    )
    attended = (
        (weighted_sum / jnp.sqrt(length.astype(jnp.float32)))
        .reshape(cand_dev, d_model)
        .astype(jnp.bfloat16)
    )
    pre_act = jnp.dot(cand_emb, tower_in[:d_model], preferred_element_type=jnp.float32) + jnp.dot(
        attended, tower_in[d_model:], preferred_element_type=jnp.float32
    )
    hidden = jax.nn.silu(pre_act).astype(jnp.bfloat16)
    return jnp.dot(hidden, tower_out, preferred_element_type=jnp.float32)[None, :]


def solution(mesh):
    placed = (
        P("req", None),
        P("req", "cand", None),
        P("req", "cand"),
        P("req", "cand", None),
        P("req", "cand"),
        P("req"),
        P(),
        P(),
        P(),
        P(),
        P(),
    )
    return jax.shard_map(
        body, mesh=mesh, in_specs=placed, out_specs=P("req", "cand"), check_vma=False
    )
```

```python
import math

import jax
import jax.numpy as jnp
from jax import lax
from jax.sharding import PartitionSpec as P

HEADS = 4


def slot_index(shard_ids, slot_count):
    count = shard_ids.shape[0]
    earlier = lax.broadcasted_iota(jnp.int32, (count, count), 1) < lax.broadcasted_iota(
        jnp.int32, (count, count), 0
    )
    same = (shard_ids[:, None] == shard_ids[None, :]) & earlier
    rank = jnp.sum(same.astype(jnp.int32), axis=1)
    return shard_ids * slot_count + rank


def select_rows(slots, n_slots):
    return (slots[:, None] == lax.broadcasted_iota(jnp.int32, (slots.shape[0], n_slots), 1)).astype(
        jnp.bfloat16
    )


def gather_over_cand(rows):
    n_cand = lax.axis_size("cand")
    me = lax.axis_index("cand")
    blocks, sources = [rows], [me]
    for hop in range(2, n_cand, 2):
        blocks.append(lax.ppermute(rows, "cand", [(i, (i + hop) % n_cand) for i in range(n_cand)]))
        sources.append((me - hop) % n_cand)
    mine = jnp.stack(blocks, axis=0)
    partner = lax.ppermute(mine, "cand", [(i, i ^ 1) for i in range(n_cand)])
    held = jnp.concatenate([mine, partner], axis=0)
    source = jnp.stack(sources)
    source = jnp.concatenate([source, source ^ 1])
    order = jnp.argmax(source[None, :] == jnp.arange(n_cand)[:, None], axis=1)
    return jnp.take(held, order, axis=0).reshape(-1, rows.shape[1])


def wanted_rows(slots, n_slots, rows):
    pick_t = (lax.broadcasted_iota(jnp.int32, (n_slots, slots.shape[0]), 0) == slots[None, :]).astype(
        jnp.bfloat16
    )
    row_parts = jnp.stack([rows // 128, rows % 128], axis=1).astype(jnp.bfloat16)
    parts = jnp.dot(pick_t, row_parts, preferred_element_type=jnp.float32).astype(jnp.int32)
    return parts[:, 0] * 128 + parts[:, 1]


def swap_over_req(blocks):
    n_req = blocks.shape[0]
    swapped = [blocks[0]]
    for hop in range(1, n_req):
        swapped.append(lax.ppermute(blocks[hop], "req", [(i, i ^ hop) for i in range(n_req)]))
    return jnp.stack(swapped, axis=0)


def body(
    table,
    history_shard,
    history_row,
    candidate_shard,
    candidate_row,
    history_length,
    w_query,
    w_key,
    w_value,
    tower_in,
    tower_out,
):
    n_dest = lax.axis_size("req")
    d_model = table.shape[1]
    hist_dev = history_row.shape[1]
    cand_dev = candidate_row.shape[1]
    packed = lax.optimization_barrier(
        jnp.concatenate(
            [history_shard[0, :, 0], history_row[0], candidate_shard[0, :, 0], candidate_row[0]]
        )
    )
    hist_shards = packed[:hist_dev]
    hist_rows = packed[hist_dev : 2 * hist_dev]
    cand_shards = packed[2 * hist_dev : 2 * hist_dev + cand_dev]
    cand_rows = packed[2 * hist_dev + cand_dev :]
    hist_cap = 4 * hist_dev // n_dest
    cand_cap = 3 * cand_dev // n_dest
    assert n_dest & (n_dest - 1) == 0
    me = lax.axis_index("req")
    hist_slot = slot_index(hist_shards ^ me, hist_cap)
    cand_slot = slot_index(cand_shards ^ me, cand_cap)
    hist_pick = select_rows(hist_slot, n_dest * hist_cap)
    cand_pick = select_rows(cand_slot, n_dest * cand_cap)
    hist_wanted = wanted_rows(hist_slot, n_dest * hist_cap, hist_rows).reshape(n_dest, hist_cap)
    cand_wanted = wanted_rows(cand_slot, n_dest * cand_cap, cand_rows).reshape(n_dest, cand_cap)
    asked = swap_over_req(jnp.concatenate([hist_wanted, cand_wanted], axis=1))
    fetched = jnp.take(table, asked.reshape(-1), axis=0, mode="clip").reshape(
        n_dest, hist_cap + cand_cap, d_model
    )
    hist_replies = swap_over_req(fetched[:, :hist_cap]).reshape(n_dest * hist_cap, d_model)
    cand_replies = swap_over_req(fetched[:, hist_cap:]).reshape(n_dest * cand_cap, d_model)
    hist_emb = jnp.dot(hist_pick, hist_replies, preferred_element_type=jnp.float32).astype(jnp.bfloat16)
    cand_emb = jnp.dot(cand_pick, cand_replies, preferred_element_type=jnp.float32).astype(jnp.bfloat16)
    head_size = d_model // HEADS
    scale_factor = 1.0 / math.sqrt(head_size)
    length = history_length[0]
    w_pair = jnp.concatenate([w_key, w_value], axis=1)
    query_row_matrix = jnp.dot(cand_emb, w_query, preferred_element_type=jnp.float32).astype(
        jnp.bfloat16
    )
    query_row_matrix = query_row_matrix.reshape(cand_dev, HEADS, head_size)
    hist_all = gather_over_cand(hist_emb)
    pair_rows = jnp.dot(hist_all, w_pair, preferred_element_type=jnp.float32).astype(jnp.bfloat16)
    count = pair_rows.shape[0]
    key_portion_slice = pair_rows[:, :d_model].reshape(count, HEADS, head_size)
    value_portion_slice = pair_rows[:, d_model:].reshape(count, HEADS, head_size)
    score_matrix = (
        jnp.einsum(
            "zun,aun->zua", query_row_matrix, key_portion_slice, preferred_element_type=jnp.float32
        )
        * scale_factor
    )
    live_mask = jnp.arange(count, dtype=jnp.int32) < length
    gate_weights = jnp.where(
        live_mask[None, None, :], jax.nn.sigmoid(score_matrix), jnp.float32(0.0)
    ).astype(jnp.bfloat16)
    weighted_sum = jnp.einsum(
        "bgo,ogl->bgl", gate_weights, value_portion_slice, preferred_element_type=jnp.float32
    )
    attended = (
        (weighted_sum / jnp.sqrt(length.astype(jnp.float32)))
        .reshape(cand_dev, d_model)
        .astype(jnp.bfloat16)
    )
    pre_act = jnp.dot(cand_emb, tower_in[:d_model], preferred_element_type=jnp.float32) + jnp.dot(
        attended, tower_in[d_model:], preferred_element_type=jnp.float32
    )
    hidden = jax.nn.silu(pre_act).astype(jnp.bfloat16)
    return jnp.dot(hidden, tower_out, preferred_element_type=jnp.float32)[None, :]


def solution(mesh):
    placed = (
        P("req", None),
        P("req", "cand", None),
        P("req", "cand"),
        P("req", "cand", None),
        P("req", "cand"),
        P("req"),
        P(),
        P(),
        P(),
        P(),
        P(),
    )
    return jax.shard_map(
        body, mesh=mesh, in_specs=placed, out_specs=P("req", "cand"), check_vma=False
    )
```

```python
import math

import jax
import jax.numpy as jnp
from jax import lax
from jax.sharding import PartitionSpec as P

HEADS = 4


def slot_index(shard_ids, slot_count):
    count = shard_ids.shape[0]
    earlier = lax.broadcasted_iota(jnp.int32, (count, count), 1) < lax.broadcasted_iota(
        jnp.int32, (count, count), 0
    )
    same = (shard_ids[:, None] == shard_ids[None, :]) & earlier
    rank = jnp.sum(same.astype(jnp.int32), axis=1)
    return shard_ids * slot_count + rank


def select_rows(slots, n_slots):
    return (slots[:, None] == lax.broadcasted_iota(jnp.int32, (slots.shape[0], n_slots), 1)).astype(
        jnp.bfloat16
    )


def gather_over_cand(rows):
    n_cand = lax.axis_size("cand")
    me = lax.axis_index("cand")
    blocks, sources = [rows], [me]
    for hop in range(2, n_cand, 2):
        blocks.append(lax.ppermute(rows, "cand", [(i, (i + hop) % n_cand) for i in range(n_cand)]))
        sources.append((me - hop) % n_cand)
    mine = jnp.stack(blocks, axis=0)
    partner = lax.ppermute(mine, "cand", [(i, i ^ 1) for i in range(n_cand)])
    source = jnp.stack(sources)
    return (mine, source), (partner, source ^ 1)


def attend(query, blocks, sources, w_pair, length, scale_factor):
    n_blocks, block_rows, d_model = blocks.shape
    count = n_blocks * block_rows
    head_size = d_model // HEADS
    pair_rows = jnp.dot(
        blocks.reshape(count, d_model), w_pair, preferred_element_type=jnp.float32
    ).astype(jnp.bfloat16)
    keys = pair_rows[:, :d_model].reshape(count, HEADS, head_size)
    values = pair_rows[:, d_model:].reshape(count, HEADS, head_size)
    scores = jnp.einsum("zun,aun->zua", query, keys, preferred_element_type=jnp.float32) * scale_factor
    position = (sources[:, None] * block_rows + jnp.arange(block_rows, dtype=jnp.int32)[None, :]).reshape(
        count
    )
    gates = jnp.where(
        (position < length)[None, None, :], jax.nn.sigmoid(scores), jnp.float32(0.0)
    ).astype(jnp.bfloat16)
    return jnp.einsum("bgo,ogl->bgl", gates, values, preferred_element_type=jnp.float32)


def wanted_rows(slots, n_slots, rows):
    pick_t = (lax.broadcasted_iota(jnp.int32, (n_slots, slots.shape[0]), 0) == slots[None, :]).astype(
        jnp.bfloat16
    )
    row_parts = jnp.stack([rows // 128, rows % 128], axis=1).astype(jnp.bfloat16)
    parts = jnp.dot(pick_t, row_parts, preferred_element_type=jnp.float32).astype(jnp.int32)
    return parts[:, 0] * 128 + parts[:, 1]


def swap_over_req(blocks):
    n_req = blocks.shape[0]
    swapped = [blocks[0]]
    for hop in range(1, n_req):
        swapped.append(lax.ppermute(blocks[hop], "req", [(i, i ^ hop) for i in range(n_req)]))
    return jnp.stack(swapped, axis=0)


def body(
    table,
    history_shard,
    history_row,
    candidate_shard,
    candidate_row,
    history_length,
    w_query,
    w_key,
    w_value,
    tower_in,
    tower_out,
):
    n_dest = lax.axis_size("req")
    d_model = table.shape[1]
    hist_dev = history_row.shape[1]
    cand_dev = candidate_row.shape[1]
    packed = lax.optimization_barrier(
        jnp.concatenate(
            [history_shard[0, :, 0], history_row[0], candidate_shard[0, :, 0], candidate_row[0]]
        )
    )
    hist_shards = packed[:hist_dev]
    hist_rows = packed[hist_dev : 2 * hist_dev]
    cand_shards = packed[2 * hist_dev : 2 * hist_dev + cand_dev]
    cand_rows = packed[2 * hist_dev + cand_dev :]
    hist_cap = 4 * hist_dev // n_dest
    cand_cap = 3 * cand_dev // n_dest
    assert n_dest & (n_dest - 1) == 0
    me = lax.axis_index("req")
    hist_slot = slot_index(hist_shards ^ me, hist_cap)
    cand_slot = slot_index(cand_shards ^ me, cand_cap)
    hist_pick = select_rows(hist_slot, n_dest * hist_cap)
    cand_pick = select_rows(cand_slot, n_dest * cand_cap)
    hist_wanted = wanted_rows(hist_slot, n_dest * hist_cap, hist_rows).reshape(n_dest, hist_cap)
    cand_wanted = wanted_rows(cand_slot, n_dest * cand_cap, cand_rows).reshape(n_dest, cand_cap)
    asked = swap_over_req(jnp.concatenate([hist_wanted, cand_wanted], axis=1))
    fetched = jnp.take(table, asked.reshape(-1), axis=0, mode="clip").reshape(
        n_dest, hist_cap + cand_cap, d_model
    )
    hist_replies = swap_over_req(fetched[:, :hist_cap]).reshape(n_dest * hist_cap, d_model)
    cand_replies = swap_over_req(fetched[:, hist_cap:]).reshape(n_dest * cand_cap, d_model)
    hist_emb = jnp.dot(hist_pick, hist_replies, preferred_element_type=jnp.float32).astype(jnp.bfloat16)
    cand_emb = jnp.dot(cand_pick, cand_replies, preferred_element_type=jnp.float32).astype(jnp.bfloat16)
    head_size = d_model // HEADS
    scale_factor = 1.0 / math.sqrt(head_size)
    length = history_length[0]
    w_pair = jnp.concatenate([w_key, w_value], axis=1)
    query_row_matrix = jnp.dot(cand_emb, w_query, preferred_element_type=jnp.float32).astype(
        jnp.bfloat16
    )
    query_row_matrix = query_row_matrix.reshape(cand_dev, HEADS, head_size)
    halves = gather_over_cand(hist_emb)
    weighted_sum = sum(
        attend(query_row_matrix, blocks, sources, w_pair, length, scale_factor)
        for blocks, sources in halves
    )
    attended = (
        (weighted_sum / jnp.sqrt(length.astype(jnp.float32)))
        .reshape(cand_dev, d_model)
        .astype(jnp.bfloat16)
    )
    pre_act = jnp.dot(cand_emb, tower_in[:d_model], preferred_element_type=jnp.float32) + jnp.dot(
        attended, tower_in[d_model:], preferred_element_type=jnp.float32
    )
    hidden = jax.nn.silu(pre_act).astype(jnp.bfloat16)
    return jnp.dot(hidden, tower_out, preferred_element_type=jnp.float32)[None, :]


def solution(mesh):
    placed = (
        P("req", None),
        P("req", "cand", None),
        P("req", "cand"),
        P("req", "cand", None),
        P("req", "cand"),
        P("req"),
        P(),
        P(),
        P(),
        P(),
        P(),
    )
    return jax.shard_map(
        body, mesh=mesh, in_specs=placed, out_specs=P("req", "cand"), check_vma=False
    )
```

```python
import math

import jax
import jax.numpy as jnp
from jax import lax
from jax.sharding import PartitionSpec as P

HEADS = 4


def slot_index(shard_ids, slot_count):
    count = shard_ids.shape[0]
    earlier = lax.broadcasted_iota(jnp.int32, (count, count), 1) < lax.broadcasted_iota(
        jnp.int32, (count, count), 0
    )
    same = (shard_ids[:, None] == shard_ids[None, :]) & earlier
    rank = jnp.sum(same.astype(jnp.int32), axis=1)
    return shard_ids * slot_count + rank


def select_rows(slots, n_slots):
    return (slots[:, None] == lax.broadcasted_iota(jnp.int32, (slots.shape[0], n_slots), 1)).astype(
        jnp.bfloat16
    )


def gather_over_cand(rows):
    n_cand = lax.axis_size("cand")
    me = lax.axis_index("cand")
    blocks, sources = [rows], [me]
    for hop in range(2, n_cand, 2):
        blocks.append(lax.ppermute(rows, "cand", [(i, (i + hop) % n_cand) for i in range(n_cand)]))
        sources.append((me - hop) % n_cand)
    mine = jnp.stack(blocks, axis=0)
    partner = lax.ppermute(mine, "cand", [(i, i ^ 1) for i in range(n_cand)])
    source = jnp.stack(sources)
    return (mine, source), (partner, source ^ 1)


def attend(query, blocks, sources, w_pair, length, scale_factor):
    n_blocks, block_rows, d_model = blocks.shape
    count = n_blocks * block_rows
    head_size = d_model // HEADS
    pair_rows = jnp.dot(
        blocks.reshape(count, d_model), w_pair, preferred_element_type=jnp.float32
    ).astype(jnp.bfloat16)
    keys = pair_rows[:, :d_model].reshape(count, HEADS, head_size)
    values = pair_rows[:, d_model:].reshape(count, HEADS, head_size)
    scores = jnp.einsum("zun,aun->zua", query, keys, preferred_element_type=jnp.float32) * scale_factor
    position = (sources[:, None] * block_rows + jnp.arange(block_rows, dtype=jnp.int32)[None, :]).reshape(
        count
    )
    gates = jnp.where(
        (position < length)[None, None, :], jax.nn.sigmoid(scores), jnp.float32(0.0)
    ).astype(jnp.bfloat16)
    return jnp.einsum("bgo,ogl->bgl", gates, values, preferred_element_type=jnp.float32)


def wanted_rows(slots, n_slots, rows):
    pick_t = (lax.broadcasted_iota(jnp.int32, (n_slots, slots.shape[0]), 0) == slots[None, :]).astype(
        jnp.bfloat16
    )
    row_parts = jnp.stack([rows // 128, rows % 128], axis=1).astype(jnp.bfloat16)
    parts = jnp.dot(pick_t, row_parts, preferred_element_type=jnp.float32).astype(jnp.int32)
    return parts[:, 0] * 128 + parts[:, 1]


def swap_over_req(blocks):
    n_req = blocks.shape[0]
    swapped = [blocks[0]]
    for hop in range(1, n_req):
        swapped.append(lax.ppermute(blocks[hop], "req", [(i, i ^ hop) for i in range(n_req)]))
    return jnp.stack(swapped, axis=0)


def body(
    table,
    history_shard,
    history_row,
    candidate_shard,
    candidate_row,
    history_length,
    w_query,
    w_key,
    w_value,
    tower_in,
    tower_out,
):
    n_dest = lax.axis_size("req")
    d_model = table.shape[1]
    hist_dev = history_row.shape[1]
    cand_dev = candidate_row.shape[1]
    packed = lax.optimization_barrier(
        jnp.concatenate(
            [history_shard[0, :, 0], history_row[0], candidate_shard[0, :, 0], candidate_row[0]]
        )
    )
    hist_shards = packed[:hist_dev]
    hist_rows = packed[hist_dev : 2 * hist_dev]
    cand_shards = packed[2 * hist_dev : 2 * hist_dev + cand_dev]
    cand_rows = packed[2 * hist_dev + cand_dev :]
    hist_cap = 4 * hist_dev // n_dest
    cand_cap = 3 * cand_dev // n_dest
    assert n_dest & (n_dest - 1) == 0
    me = lax.axis_index("req")
    hist_slot = slot_index(hist_shards ^ me, hist_cap)
    cand_slot = slot_index(cand_shards ^ me, cand_cap)
    hist_pick = select_rows(hist_slot, n_dest * hist_cap)
    cand_pick = select_rows(cand_slot, n_dest * cand_cap)
    hist_wanted = wanted_rows(hist_slot, n_dest * hist_cap, hist_rows).reshape(n_dest, hist_cap)
    cand_wanted = wanted_rows(cand_slot, n_dest * cand_cap, cand_rows).reshape(n_dest, cand_cap)
    asked = swap_over_req(jnp.concatenate([hist_wanted, cand_wanted], axis=1))
    fetched = jnp.take(table, asked.reshape(-1), axis=0, mode="clip").reshape(
        n_dest, hist_cap + cand_cap, d_model
    )
    hist_replies = swap_over_req(fetched[:, :hist_cap]).reshape(n_dest * hist_cap, d_model)
    cand_replies = swap_over_req(fetched[:, hist_cap:]).reshape(n_dest * cand_cap, d_model)
    hist_emb = jnp.dot(hist_pick, hist_replies, preferred_element_type=jnp.float32).astype(jnp.bfloat16)
    cand_emb = jnp.dot(cand_pick, cand_replies, preferred_element_type=jnp.float32).astype(jnp.bfloat16)
    head_size = d_model // HEADS
    scale_factor = 1.0 / math.sqrt(head_size)
    length = history_length[0]
    w_pair = jnp.concatenate([w_key, w_value], axis=1)
    query_row_matrix = jnp.dot(cand_emb, w_query, preferred_element_type=jnp.float32).astype(
        jnp.bfloat16
    )
    query_row_matrix = query_row_matrix.reshape(cand_dev, HEADS, head_size)
    (mine, mine_sources), (partner, partner_sources) = gather_over_cand(hist_emb)
    weighted_sum = attend(
        query_row_matrix,
        jnp.concatenate([mine, partner], axis=0),
        jnp.concatenate([mine_sources, partner_sources]),
        w_pair,
        length,
        scale_factor,
    )
    attended = (
        (weighted_sum / jnp.sqrt(length.astype(jnp.float32)))
        .reshape(cand_dev, d_model)
        .astype(jnp.bfloat16)
    )
    pre_act = jnp.dot(cand_emb, tower_in[:d_model], preferred_element_type=jnp.float32) + jnp.dot(
        attended, tower_in[d_model:], preferred_element_type=jnp.float32
    )
    hidden = jax.nn.silu(pre_act).astype(jnp.bfloat16)
    return jnp.dot(hidden, tower_out, preferred_element_type=jnp.float32)[None, :]


def solution(mesh):
    placed = (
        P("req", None),
        P("req", "cand", None),
        P("req", "cand"),
        P("req", "cand", None),
        P("req", "cand"),
        P("req"),
        P(),
        P(),
        P(),
        P(),
        P(),
    )
    return jax.shard_map(
        body, mesh=mesh, in_specs=placed, out_specs=P("req", "cand"), check_vma=False
    )
```

```python
import math

import jax
import jax.numpy as jnp
from jax import lax
from jax.sharding import PartitionSpec as P

HEADS = 4


def slot_index(shard_ids, slot_count):
    count = shard_ids.shape[0]
    earlier = lax.broadcasted_iota(jnp.int32, (count, count), 1) < lax.broadcasted_iota(
        jnp.int32, (count, count), 0
    )
    same = (shard_ids[:, None] == shard_ids[None, :]) & earlier
    rank = jnp.sum(same.astype(jnp.int32), axis=1)
    return shard_ids * slot_count + rank


def select_rows(slots, n_slots):
    return (slots[:, None] == lax.broadcasted_iota(jnp.int32, (slots.shape[0], n_slots), 1)).astype(
        jnp.bfloat16
    )


def gather_over_cand(rows):
    n_cand = lax.axis_size("cand")
    me = lax.axis_index("cand")
    blocks, sources = [rows], [me]
    for hop in range(2, n_cand, 2):
        blocks.append(lax.ppermute(rows, "cand", [(i, (i + hop) % n_cand) for i in range(n_cand)]))
        sources.append((me - hop) % n_cand)
    mine = jnp.stack(blocks, axis=0)
    partner = lax.ppermute(mine, "cand", [(i, i ^ 1) for i in range(n_cand)])
    source = jnp.stack(sources)
    return (mine, source), (partner, source ^ 1)


def logistic(x):
    return 0.5 + 0.5 * jnp.tanh(0.5 * x)


def attend(query, blocks, sources, w_pair, length, scale_factor):
    n_blocks, block_rows, d_model = blocks.shape
    count = n_blocks * block_rows
    head_size = d_model // HEADS
    pair_rows = jnp.dot(
        blocks.reshape(count, d_model), w_pair, preferred_element_type=jnp.float32
    ).astype(jnp.bfloat16)
    keys = pair_rows[:, :d_model].reshape(count, HEADS, head_size)
    values = pair_rows[:, d_model:].reshape(count, HEADS, head_size)
    scores = jnp.einsum("zun,aun->zua", query, keys, preferred_element_type=jnp.float32) * scale_factor
    position = (sources[:, None] * block_rows + jnp.arange(block_rows, dtype=jnp.int32)[None, :]).reshape(
        count
    )
    gates = jnp.where(
        (position < length)[None, None, :], logistic(scores), jnp.float32(0.0)
    ).astype(jnp.bfloat16)
    return jnp.einsum("bgo,ogl->bgl", gates, values, preferred_element_type=jnp.float32)


def wanted_rows(slots, n_slots, rows):
    pick_t = (lax.broadcasted_iota(jnp.int32, (n_slots, slots.shape[0]), 0) == slots[None, :]).astype(
        jnp.bfloat16
    )
    row_parts = jnp.stack([rows // 128, rows % 128], axis=1).astype(jnp.bfloat16)
    parts = jnp.dot(pick_t, row_parts, preferred_element_type=jnp.float32).astype(jnp.int32)
    return parts[:, 0] * 128 + parts[:, 1]


def swap_over_req(blocks):
    n_req = blocks.shape[0]
    swapped = [blocks[0]]
    for hop in range(1, n_req):
        swapped.append(lax.ppermute(blocks[hop], "req", [(i, i ^ hop) for i in range(n_req)]))
    return jnp.stack(swapped, axis=0)


def body(
    table,
    history_shard,
    history_row,
    candidate_shard,
    candidate_row,
    history_length,
    w_query,
    w_key,
    w_value,
    tower_in,
    tower_out,
):
    n_dest = lax.axis_size("req")
    d_model = table.shape[1]
    hist_dev = history_row.shape[1]
    cand_dev = candidate_row.shape[1]
    packed = lax.optimization_barrier(
        jnp.concatenate(
            [history_shard[0, :, 0], history_row[0], candidate_shard[0, :, 0], candidate_row[0]]
        )
    )
    hist_shards = packed[:hist_dev]
    hist_rows = packed[hist_dev : 2 * hist_dev]
    cand_shards = packed[2 * hist_dev : 2 * hist_dev + cand_dev]
    cand_rows = packed[2 * hist_dev + cand_dev :]
    hist_cap = 4 * hist_dev // n_dest
    cand_cap = 3 * cand_dev // n_dest
    assert n_dest & (n_dest - 1) == 0
    me = lax.axis_index("req")
    hist_slot = slot_index(hist_shards ^ me, hist_cap)
    cand_slot = slot_index(cand_shards ^ me, cand_cap)
    hist_pick = select_rows(hist_slot, n_dest * hist_cap)
    cand_pick = select_rows(cand_slot, n_dest * cand_cap)
    hist_wanted = wanted_rows(hist_slot, n_dest * hist_cap, hist_rows).reshape(n_dest, hist_cap)
    cand_wanted = wanted_rows(cand_slot, n_dest * cand_cap, cand_rows).reshape(n_dest, cand_cap)
    asked = swap_over_req(jnp.concatenate([hist_wanted, cand_wanted], axis=1))
    fetched = jnp.take(table, asked.reshape(-1), axis=0, mode="clip").reshape(
        n_dest, hist_cap + cand_cap, d_model
    )
    hist_replies = swap_over_req(fetched[:, :hist_cap]).reshape(n_dest * hist_cap, d_model)
    cand_replies = swap_over_req(fetched[:, hist_cap:]).reshape(n_dest * cand_cap, d_model)
    hist_emb = jnp.dot(hist_pick, hist_replies, preferred_element_type=jnp.float32).astype(jnp.bfloat16)
    cand_emb = jnp.dot(cand_pick, cand_replies, preferred_element_type=jnp.float32).astype(jnp.bfloat16)
    head_size = d_model // HEADS
    scale_factor = 1.0 / math.sqrt(head_size)
    length = history_length[0]
    w_pair = jnp.concatenate([w_key, w_value], axis=1)
    query_row_matrix = jnp.dot(cand_emb, w_query, preferred_element_type=jnp.float32).astype(
        jnp.bfloat16
    )
    query_row_matrix = query_row_matrix.reshape(cand_dev, HEADS, head_size)
    (mine, mine_sources), (partner, partner_sources) = gather_over_cand(hist_emb)
    weighted_sum = attend(
        query_row_matrix,
        jnp.concatenate([mine, partner], axis=0),
        jnp.concatenate([mine_sources, partner_sources]),
        w_pair,
        length,
        scale_factor,
    )
    attended = (
        (weighted_sum / jnp.sqrt(length.astype(jnp.float32)))
        .reshape(cand_dev, d_model)
        .astype(jnp.bfloat16)
    )
    pre_act = jnp.dot(cand_emb, tower_in[:d_model], preferred_element_type=jnp.float32) + jnp.dot(
        attended, tower_in[d_model:], preferred_element_type=jnp.float32
    )
    hidden = (pre_act * logistic(pre_act)).astype(jnp.bfloat16)
    return jnp.dot(hidden, tower_out, preferred_element_type=jnp.float32)[None, :]


def solution(mesh):
    placed = (
        P("req", None),
        P("req", "cand", None),
        P("req", "cand"),
        P("req", "cand", None),
        P("req", "cand"),
        P("req"),
        P(),
        P(),
        P(),
        P(),
        P(),
    )
    return jax.shard_map(
        body, mesh=mesh, in_specs=placed, out_specs=P("req", "cand"), check_vma=False
    )
```

```python
import math

import jax
import jax.numpy as jnp
from jax import lax
from jax.sharding import PartitionSpec as P

HEADS = 4


def slot_index(shard_ids, slot_count):
    count = shard_ids.shape[0]
    earlier = lax.broadcasted_iota(jnp.int32, (count, count), 1) < lax.broadcasted_iota(
        jnp.int32, (count, count), 0
    )
    same = (shard_ids[:, None] == shard_ids[None, :]) & earlier
    rank = jnp.sum(same.astype(jnp.int32), axis=1)
    return shard_ids * slot_count + rank


def select_rows(slots, n_slots):
    return (slots[:, None] == lax.broadcasted_iota(jnp.int32, (slots.shape[0], n_slots), 1)).astype(
        jnp.bfloat16
    )


def gather_over_cand(rows):
    n_cand = lax.axis_size("cand")
    me = lax.axis_index("cand")
    blocks, sources = [rows], [me]
    for hop in range(2, n_cand, 2):
        blocks.append(lax.ppermute(rows, "cand", [(i, (i + hop) % n_cand) for i in range(n_cand)]))
        sources.append((me - hop) % n_cand)
    mine = jnp.stack(blocks, axis=0)
    partner = lax.ppermute(mine, "cand", [(i, i ^ 1) for i in range(n_cand)])
    source = jnp.stack(sources)
    return (mine, source), (partner, source ^ 1)


def logistic(x):
    return 0.5 + 0.5 * jnp.tanh(0.5 * x)


def project(blocks, w_pair):
    n_blocks, block_rows, d_model = blocks.shape
    return jnp.dot(
        blocks.reshape(n_blocks * block_rows, d_model), w_pair, preferred_element_type=jnp.float32
    ).astype(jnp.bfloat16)


def attend(query, pair_rows, sources, block_rows, length, scale_factor):
    count, d_model = pair_rows.shape[0], pair_rows.shape[1] // 2
    head_size = d_model // HEADS
    keys = pair_rows[:, :d_model].reshape(count, HEADS, head_size)
    values = pair_rows[:, d_model:].reshape(count, HEADS, head_size)
    scores = jnp.einsum("zun,aun->zua", query, keys, preferred_element_type=jnp.float32) * scale_factor
    position = (sources[:, None] * block_rows + jnp.arange(block_rows, dtype=jnp.int32)[None, :]).reshape(
        count
    )
    gates = jnp.where(
        (position < length)[None, None, :], logistic(scores), jnp.float32(0.0)
    ).astype(jnp.bfloat16)
    return jnp.einsum("bgo,ogl->bgl", gates, values, preferred_element_type=jnp.float32)


def wanted_rows(slots, n_slots, rows):
    pick_t = (lax.broadcasted_iota(jnp.int32, (n_slots, slots.shape[0]), 0) == slots[None, :]).astype(
        jnp.bfloat16
    )
    row_parts = jnp.stack([rows // 128, rows % 128], axis=1).astype(jnp.bfloat16)
    parts = jnp.dot(pick_t, row_parts, preferred_element_type=jnp.float32).astype(jnp.int32)
    return parts[:, 0] * 128 + parts[:, 1]


def swap_over_req(blocks):
    n_req = blocks.shape[0]
    swapped = [blocks[0]]
    for hop in range(1, n_req):
        swapped.append(lax.ppermute(blocks[hop], "req", [(i, i ^ hop) for i in range(n_req)]))
    return jnp.stack(swapped, axis=0)


def body(
    table,
    history_shard,
    history_row,
    candidate_shard,
    candidate_row,
    history_length,
    w_query,
    w_key,
    w_value,
    tower_in,
    tower_out,
):
    n_dest = lax.axis_size("req")
    d_model = table.shape[1]
    hist_dev = history_row.shape[1]
    cand_dev = candidate_row.shape[1]
    packed = lax.optimization_barrier(
        jnp.concatenate(
            [history_shard[0, :, 0], history_row[0], candidate_shard[0, :, 0], candidate_row[0]]
        )
    )
    hist_shards = packed[:hist_dev]
    hist_rows = packed[hist_dev : 2 * hist_dev]
    cand_shards = packed[2 * hist_dev : 2 * hist_dev + cand_dev]
    cand_rows = packed[2 * hist_dev + cand_dev :]
    hist_cap = 4 * hist_dev // n_dest
    cand_cap = 3 * cand_dev // n_dest
    assert n_dest & (n_dest - 1) == 0
    me = lax.axis_index("req")
    hist_slot = slot_index(hist_shards ^ me, hist_cap)
    cand_slot = slot_index(cand_shards ^ me, cand_cap)
    hist_pick = select_rows(hist_slot, n_dest * hist_cap)
    cand_pick = select_rows(cand_slot, n_dest * cand_cap)
    hist_wanted = wanted_rows(hist_slot, n_dest * hist_cap, hist_rows).reshape(n_dest, hist_cap)
    cand_wanted = wanted_rows(cand_slot, n_dest * cand_cap, cand_rows).reshape(n_dest, cand_cap)
    asked = swap_over_req(jnp.concatenate([hist_wanted, cand_wanted], axis=1))
    fetched = jnp.take(table, asked.reshape(-1), axis=0, mode="clip").reshape(
        n_dest, hist_cap + cand_cap, d_model
    )
    hist_replies = swap_over_req(fetched[:, :hist_cap]).reshape(n_dest * hist_cap, d_model)
    cand_replies = swap_over_req(fetched[:, hist_cap:]).reshape(n_dest * cand_cap, d_model)
    hist_emb = jnp.dot(hist_pick, hist_replies, preferred_element_type=jnp.float32).astype(jnp.bfloat16)
    cand_emb = jnp.dot(cand_pick, cand_replies, preferred_element_type=jnp.float32).astype(jnp.bfloat16)
    head_size = d_model // HEADS
    scale_factor = 1.0 / math.sqrt(head_size)
    length = history_length[0]
    w_pair = jnp.concatenate([w_key, w_value], axis=1)
    query_row_matrix = jnp.dot(cand_emb, w_query, preferred_element_type=jnp.float32).astype(
        jnp.bfloat16
    )
    query_row_matrix = query_row_matrix.reshape(cand_dev, HEADS, head_size)
    (mine, mine_sources), (partner, partner_sources) = gather_over_cand(hist_emb)
    weighted_sum = attend(
        query_row_matrix,
        jnp.concatenate([project(mine, w_pair), project(partner, w_pair)], axis=0),
        jnp.concatenate([mine_sources, partner_sources]),
        hist_dev,
        length,
        scale_factor,
    )
    attended = (
        (weighted_sum / jnp.sqrt(length.astype(jnp.float32)))
        .reshape(cand_dev, d_model)
        .astype(jnp.bfloat16)
    )
    pre_act = jnp.dot(cand_emb, tower_in[:d_model], preferred_element_type=jnp.float32) + jnp.dot(
        attended, tower_in[d_model:], preferred_element_type=jnp.float32
    )
    hidden = (pre_act * logistic(pre_act)).astype(jnp.bfloat16)
    return jnp.dot(hidden, tower_out, preferred_element_type=jnp.float32)[None, :]


def solution(mesh):
    placed = (
        P("req", None),
        P("req", "cand", None),
        P("req", "cand"),
        P("req", "cand", None),
        P("req", "cand"),
        P("req"),
        P(),
        P(),
        P(),
        P(),
        P(),
    )
    return jax.shard_map(
        body, mesh=mesh, in_specs=placed, out_specs=P("req", "cand"), check_vma=False
    )
```

```python
import math

import jax
import jax.numpy as jnp
from jax import lax
from jax.sharding import PartitionSpec as P

HEADS = 4


def slot_index(shard_ids, slot_count):
    count = shard_ids.shape[0]
    earlier = lax.broadcasted_iota(jnp.int32, (count, count), 1) < lax.broadcasted_iota(
        jnp.int32, (count, count), 0
    )
    same = (shard_ids[:, None] == shard_ids[None, :]) & earlier
    rank = jnp.sum(same.astype(jnp.int32), axis=1)
    return shard_ids * slot_count + rank


def select_rows(slots, n_slots):
    return (slots[:, None] == lax.broadcasted_iota(jnp.int32, (slots.shape[0], n_slots), 1)).astype(
        jnp.bfloat16
    )


def gather_over_cand(rows):
    n_cand = lax.axis_size("cand")
    me = lax.axis_index("cand")
    blocks, sources = [rows], [me]
    for hop in range(2, n_cand, 2):
        blocks.append(lax.ppermute(rows, "cand", [(i, (i + hop) % n_cand) for i in range(n_cand)]))
        sources.append((me - hop) % n_cand)
    mine = jnp.stack(blocks, axis=0)
    partner = lax.ppermute(mine, "cand", [(i, i ^ 1) for i in range(n_cand)])
    source = jnp.stack(sources)
    return (mine, source), (partner, source ^ 1)


def logistic(x):
    return 0.5 + 0.5 * jnp.tanh(0.5 * x)


def attend(query, blocks, sources, w_pair, length, scale_factor):
    n_blocks, block_rows, d_model = blocks.shape
    count = n_blocks * block_rows
    head_size = d_model // HEADS
    pair_rows = jnp.dot(
        blocks.reshape(count, d_model), w_pair, preferred_element_type=jnp.float32
    ).astype(jnp.bfloat16)
    keys = pair_rows[:, :d_model].reshape(count, HEADS, head_size)
    values = pair_rows[:, d_model:].reshape(count, HEADS, head_size)
    scores = jnp.einsum("zun,aun->zua", query, keys, preferred_element_type=jnp.float32) * scale_factor
    position = (sources[:, None] * block_rows + jnp.arange(block_rows, dtype=jnp.int32)[None, :]).reshape(
        count
    )
    gates = jnp.where(
        (position < length)[None, None, :], logistic(scores), jnp.float32(0.0)
    ).astype(jnp.bfloat16)
    return jnp.einsum("bgo,ogl->bgl", gates, values, preferred_element_type=jnp.float32)


def wanted_rows(slots, n_slots, rows):
    pick_t = (lax.broadcasted_iota(jnp.int32, (n_slots, slots.shape[0]), 0) == slots[None, :]).astype(
        jnp.bfloat16
    )
    row_parts = jnp.stack([rows // 128, rows % 128], axis=1).astype(jnp.bfloat16)
    parts = jnp.dot(pick_t, row_parts, preferred_element_type=jnp.float32).astype(jnp.int32)
    return parts[:, 0] * 128 + parts[:, 1]


def swap_over_req(blocks):
    n_req = blocks.shape[0]
    swapped = [blocks[0]]
    for hop in range(1, n_req):
        swapped.append(lax.ppermute(blocks[hop], "req", [(i, i ^ hop) for i in range(n_req)]))
    return jnp.stack(swapped, axis=0)


def body(
    table,
    history_shard,
    history_row,
    candidate_shard,
    candidate_row,
    history_length,
    w_query,
    w_key,
    w_value,
    tower_in,
    tower_out,
):
    n_dest = lax.axis_size("req")
    d_model = table.shape[1]
    hist_dev = history_row.shape[1]
    cand_dev = candidate_row.shape[1]
    packed = lax.optimization_barrier(
        jnp.concatenate(
            [history_shard[0, :, 0], history_row[0], candidate_shard[0, :, 0], candidate_row[0]]
        )
    )
    hist_shards = packed[:hist_dev]
    hist_rows = packed[hist_dev : 2 * hist_dev]
    cand_shards = packed[2 * hist_dev : 2 * hist_dev + cand_dev]
    cand_rows = packed[2 * hist_dev + cand_dev :]
    hist_cap = 4 * hist_dev // n_dest
    cand_cap = 3 * cand_dev // n_dest
    assert n_dest & (n_dest - 1) == 0
    me = lax.axis_index("req")
    hist_slot = slot_index(hist_shards ^ me, hist_cap)
    cand_slot = slot_index(cand_shards ^ me, cand_cap)
    hist_pick = select_rows(hist_slot, n_dest * hist_cap)
    cand_pick = select_rows(cand_slot, n_dest * cand_cap)
    hist_wanted = wanted_rows(hist_slot, n_dest * hist_cap, hist_rows).reshape(n_dest, hist_cap)
    cand_wanted = wanted_rows(cand_slot, n_dest * cand_cap, cand_rows).reshape(n_dest, cand_cap)
    asked = swap_over_req(jnp.concatenate([hist_wanted, cand_wanted], axis=1))
    fetched = jnp.take(table, asked.reshape(-1), axis=0, mode="clip").reshape(
        n_dest, hist_cap + cand_cap, d_model
    )
    hist_replies = swap_over_req(fetched[:, :hist_cap]).reshape(n_dest * hist_cap, d_model)
    hist_emb = jnp.dot(hist_pick, hist_replies, preferred_element_type=jnp.float32).astype(jnp.bfloat16)
    head_size = d_model // HEADS
    scale_factor = 1.0 / math.sqrt(head_size)
    length = history_length[0]
    w_pair = jnp.concatenate([w_key, w_value], axis=1)
    (mine, mine_sources), (partner, partner_sources) = gather_over_cand(hist_emb)
    cand_sent, _ = lax.optimization_barrier((fetched[:, hist_cap:], mine[1]))
    cand_replies = swap_over_req(cand_sent).reshape(n_dest * cand_cap, d_model)
    cand_emb = jnp.dot(cand_pick, cand_replies, preferred_element_type=jnp.float32).astype(jnp.bfloat16)
    query_row_matrix = jnp.dot(cand_emb, w_query, preferred_element_type=jnp.float32).astype(
        jnp.bfloat16
    )
    query_row_matrix = query_row_matrix.reshape(cand_dev, HEADS, head_size)
    weighted_sum = attend(
        query_row_matrix,
        jnp.concatenate([mine, partner], axis=0),
        jnp.concatenate([mine_sources, partner_sources]),
        w_pair,
        length,
        scale_factor,
    )
    attended = (
        (weighted_sum / jnp.sqrt(length.astype(jnp.float32)))
        .reshape(cand_dev, d_model)
        .astype(jnp.bfloat16)
    )
    pre_act = jnp.dot(cand_emb, tower_in[:d_model], preferred_element_type=jnp.float32) + jnp.dot(
        attended, tower_in[d_model:], preferred_element_type=jnp.float32
    )
    hidden = (pre_act * logistic(pre_act)).astype(jnp.bfloat16)
    return jnp.dot(hidden, tower_out, preferred_element_type=jnp.float32)[None, :]


def solution(mesh):
    placed = (
        P("req", None),
        P("req", "cand", None),
        P("req", "cand"),
        P("req", "cand", None),
        P("req", "cand"),
        P("req"),
        P(),
        P(),
        P(),
        P(),
        P(),
    )
    return jax.shard_map(
        body, mesh=mesh, in_specs=placed, out_specs=P("req", "cand"), check_vma=False
    )
```

```python
import math

import jax
import jax.numpy as jnp
from jax import lax
from jax.sharding import PartitionSpec as P

HEADS = 4


def slot_index(shard_ids, slot_count):
    count = shard_ids.shape[0]
    earlier = lax.broadcasted_iota(jnp.int32, (count, count), 1) < lax.broadcasted_iota(
        jnp.int32, (count, count), 0
    )
    same = (shard_ids[:, None] == shard_ids[None, :]) & earlier
    rank = jnp.sum(same.astype(jnp.int32), axis=1)
    return shard_ids * slot_count + rank


def select_rows(slots, n_slots):
    return (slots[:, None] == lax.broadcasted_iota(jnp.int32, (slots.shape[0], n_slots), 1)).astype(
        jnp.bfloat16
    )


def gather_over_cand(rows):
    n_cand = lax.axis_size("cand")
    me = lax.axis_index("cand")
    blocks, sources = [rows], [me]
    for hop in range(2, n_cand, 2):
        blocks.append(lax.ppermute(rows, "cand", [(i, (i + hop) % n_cand) for i in range(n_cand)]))
        sources.append((me - hop) % n_cand)
    mine = jnp.stack(blocks, axis=0)
    partner = lax.ppermute(mine, "cand", [(i, i ^ 1) for i in range(n_cand)])
    source = jnp.stack(sources)
    return (mine, source), (partner, source ^ 1)


def logistic(x):
    return 0.5 + 0.5 * jnp.tanh(0.5 * x)


def attend(query, blocks, sources, w_pair, length, scale_factor):
    n_blocks, block_rows, d_model = blocks.shape
    count = n_blocks * block_rows
    head_size = d_model // HEADS
    pair_rows = jnp.dot(
        blocks.reshape(count, d_model), w_pair, preferred_element_type=jnp.float32
    ).astype(jnp.bfloat16)
    keys = pair_rows[:, :d_model].reshape(count, HEADS, head_size)
    values = pair_rows[:, d_model:].reshape(count, HEADS, head_size)
    scores = jnp.einsum("zun,aun->zua", query, keys, preferred_element_type=jnp.float32) * scale_factor
    position = (sources[:, None] * block_rows + jnp.arange(block_rows, dtype=jnp.int32)[None, :]).reshape(
        count
    )
    gates = jnp.where(
        (position < length)[None, None, :], logistic(scores), jnp.float32(0.0)
    ).astype(jnp.bfloat16)
    return jnp.einsum("bgo,ogl->bgl", gates, values, preferred_element_type=jnp.float32)


def wanted_rows(slots, n_slots, rows):
    pick_t = (lax.broadcasted_iota(jnp.int32, (n_slots, slots.shape[0]), 0) == slots[None, :]).astype(
        jnp.bfloat16
    )
    row_parts = jnp.stack([rows // 128, rows % 128], axis=1).astype(jnp.bfloat16)
    parts = jnp.dot(pick_t, row_parts, preferred_element_type=jnp.float32).astype(jnp.int32)
    return parts[:, 0] * 128 + parts[:, 1]


def swap_over_req(blocks):
    n_req = blocks.shape[0]
    swapped = [blocks[0]]
    for hop in range(1, n_req):
        swapped.append(lax.ppermute(blocks[hop], "req", [(i, i ^ hop) for i in range(n_req)]))
    return jnp.stack(swapped, axis=0)


def body(
    table,
    history_shard,
    history_row,
    candidate_shard,
    candidate_row,
    history_length,
    w_query,
    w_key,
    w_value,
    tower_in,
    tower_out,
):
    n_dest = lax.axis_size("req")
    d_model = table.shape[1]
    hist_dev = history_row.shape[1]
    cand_dev = candidate_row.shape[1]
    packed = lax.optimization_barrier(
        jnp.concatenate(
            [history_shard[0, :, 0], history_row[0], candidate_shard[0, :, 0], candidate_row[0]]
        )
    )
    hist_shards = packed[:hist_dev]
    hist_rows = packed[hist_dev : 2 * hist_dev]
    cand_shards = packed[2 * hist_dev : 2 * hist_dev + cand_dev]
    cand_rows = packed[2 * hist_dev + cand_dev :]
    hist_cap = 4 * hist_dev // n_dest
    cand_cap = 3 * cand_dev // n_dest
    assert n_dest & (n_dest - 1) == 0
    me = lax.axis_index("req")
    hist_slot = slot_index(hist_shards ^ me, hist_cap)
    cand_slot = slot_index(cand_shards ^ me, cand_cap)
    hist_pick = select_rows(hist_slot, n_dest * hist_cap)
    cand_pick = select_rows(cand_slot, n_dest * cand_cap)
    hist_wanted = wanted_rows(hist_slot, n_dest * hist_cap, hist_rows).reshape(n_dest, hist_cap)
    cand_wanted = wanted_rows(cand_slot, n_dest * cand_cap, cand_rows).reshape(n_dest, cand_cap)
    asked = swap_over_req(jnp.concatenate([hist_wanted, cand_wanted], axis=1))
    fetched = jnp.take(table, asked.reshape(-1), axis=0, mode="clip").reshape(
        n_dest, hist_cap + cand_cap, d_model
    )
    replies = swap_over_req(fetched)
    hist_replies = replies[:, :hist_cap].reshape(n_dest * hist_cap, d_model)
    cand_replies = replies[:, hist_cap:].reshape(n_dest * cand_cap, d_model)
    hist_emb = jnp.dot(hist_pick, hist_replies, preferred_element_type=jnp.float32).astype(jnp.bfloat16)
    cand_emb = jnp.dot(cand_pick, cand_replies, preferred_element_type=jnp.float32).astype(jnp.bfloat16)
    head_size = d_model // HEADS
    scale_factor = 1.0 / math.sqrt(head_size)
    length = history_length[0]
    w_pair = jnp.concatenate([w_key, w_value], axis=1)
    query_row_matrix = jnp.dot(cand_emb, w_query, preferred_element_type=jnp.float32).astype(
        jnp.bfloat16
    )
    query_row_matrix = query_row_matrix.reshape(cand_dev, HEADS, head_size)
    (mine, mine_sources), (partner, partner_sources) = gather_over_cand(hist_emb)
    weighted_sum = attend(
        query_row_matrix,
        jnp.concatenate([mine, partner], axis=0),
        jnp.concatenate([mine_sources, partner_sources]),
        w_pair,
        length,
        scale_factor,
    )
    attended = (
        (weighted_sum / jnp.sqrt(length.astype(jnp.float32)))
        .reshape(cand_dev, d_model)
        .astype(jnp.bfloat16)
    )
    pre_act = jnp.dot(cand_emb, tower_in[:d_model], preferred_element_type=jnp.float32) + jnp.dot(
        attended, tower_in[d_model:], preferred_element_type=jnp.float32
    )
    hidden = (pre_act * logistic(pre_act)).astype(jnp.bfloat16)
    return jnp.dot(hidden, tower_out, preferred_element_type=jnp.float32)[None, :]


def solution(mesh):
    placed = (
        P("req", None),
        P("req", "cand", None),
        P("req", "cand"),
        P("req", "cand", None),
        P("req", "cand"),
        P("req"),
        P(),
        P(),
        P(),
        P(),
        P(),
    )
    return jax.shard_map(
        body, mesh=mesh, in_specs=placed, out_specs=P("req", "cand"), check_vma=False
    )
```

```python
import math

import jax
import jax.numpy as jnp
from jax import lax
from jax.sharding import PartitionSpec as P

HEADS = 4


def slot_index(shard_ids, slot_count):
    count = shard_ids.shape[0]
    earlier = lax.broadcasted_iota(jnp.int32, (count, count), 1) < lax.broadcasted_iota(
        jnp.int32, (count, count), 0
    )
    same = (shard_ids[:, None] == shard_ids[None, :]) & earlier
    rank = jnp.sum(same.astype(jnp.int32), axis=1)
    return shard_ids * slot_count + rank


def select_rows(slots, n_slots):
    return (slots[:, None] == lax.broadcasted_iota(jnp.int32, (slots.shape[0], n_slots), 1)).astype(
        jnp.bfloat16
    )


def gather_over_cand(rows):
    n_cand = lax.axis_size("cand")
    assert n_cand & (n_cand - 1) == 0
    me = lax.axis_index("cand")
    blocks, sources = [rows], [me]
    for hop in range(2, n_cand, 2):
        blocks.append(lax.ppermute(rows, "cand", [(i, i ^ hop) for i in range(n_cand)]))
        sources.append(me ^ hop)
    mine = jnp.stack(blocks, axis=0)
    partner = lax.ppermute(mine, "cand", [(i, i ^ 1) for i in range(n_cand)])
    source = jnp.stack(sources)
    return (mine, source), (partner, source ^ 1)


def logistic(x):
    return 0.5 + 0.5 * jnp.tanh(0.5 * x)


def attend(query, blocks, sources, w_pair, length, scale_factor):
    n_blocks, block_rows, d_model = blocks.shape
    count = n_blocks * block_rows
    head_size = d_model // HEADS
    pair_rows = jnp.dot(
        blocks.reshape(count, d_model), w_pair, preferred_element_type=jnp.float32
    ).astype(jnp.bfloat16)
    keys = pair_rows[:, :d_model].reshape(count, HEADS, head_size)
    values = pair_rows[:, d_model:].reshape(count, HEADS, head_size)
    scores = jnp.einsum("zun,aun->zua", query, keys, preferred_element_type=jnp.float32) * scale_factor
    position = (sources[:, None] * block_rows + jnp.arange(block_rows, dtype=jnp.int32)[None, :]).reshape(
        count
    )
    gates = jnp.where(
        (position < length)[None, None, :], logistic(scores), jnp.float32(0.0)
    ).astype(jnp.bfloat16)
    return jnp.einsum("bgo,ogl->bgl", gates, values, preferred_element_type=jnp.float32)


def wanted_rows(slots, n_slots, rows):
    pick_t = (lax.broadcasted_iota(jnp.int32, (n_slots, slots.shape[0]), 0) == slots[None, :]).astype(
        jnp.bfloat16
    )
    row_parts = jnp.stack([rows // 128, rows % 128], axis=1).astype(jnp.bfloat16)
    parts = jnp.dot(pick_t, row_parts, preferred_element_type=jnp.float32).astype(jnp.int32)
    return parts[:, 0] * 128 + parts[:, 1]


def swap_over_req(blocks):
    n_req = blocks.shape[0]
    swapped = [blocks[0]]
    for hop in range(1, n_req):
        swapped.append(lax.ppermute(blocks[hop], "req", [(i, i ^ hop) for i in range(n_req)]))
    return jnp.stack(swapped, axis=0)


def body(
    table,
    history_shard,
    history_row,
    candidate_shard,
    candidate_row,
    history_length,
    w_query,
    w_key,
    w_value,
    tower_in,
    tower_out,
):
    n_dest = lax.axis_size("req")
    d_model = table.shape[1]
    hist_dev = history_row.shape[1]
    cand_dev = candidate_row.shape[1]
    packed = lax.optimization_barrier(
        jnp.concatenate(
            [history_shard[0, :, 0], history_row[0], candidate_shard[0, :, 0], candidate_row[0]]
        )
    )
    hist_shards = packed[:hist_dev]
    hist_rows = packed[hist_dev : 2 * hist_dev]
    cand_shards = packed[2 * hist_dev : 2 * hist_dev + cand_dev]
    cand_rows = packed[2 * hist_dev + cand_dev :]
    hist_cap = 4 * hist_dev // n_dest
    cand_cap = 3 * cand_dev // n_dest
    assert n_dest & (n_dest - 1) == 0
    me = lax.axis_index("req")
    hist_slot = slot_index(hist_shards ^ me, hist_cap)
    cand_slot = slot_index(cand_shards ^ me, cand_cap)
    hist_pick = select_rows(hist_slot, n_dest * hist_cap)
    cand_pick = select_rows(cand_slot, n_dest * cand_cap)
    hist_wanted = wanted_rows(hist_slot, n_dest * hist_cap, hist_rows).reshape(n_dest, hist_cap)
    cand_wanted = wanted_rows(cand_slot, n_dest * cand_cap, cand_rows).reshape(n_dest, cand_cap)
    asked = swap_over_req(jnp.concatenate([hist_wanted, cand_wanted], axis=1))
    fetched = jnp.take(table, asked.reshape(-1), axis=0, mode="clip").reshape(
        n_dest, hist_cap + cand_cap, d_model
    )
    hist_replies = swap_over_req(fetched[:, :hist_cap]).reshape(n_dest * hist_cap, d_model)
    cand_replies = swap_over_req(fetched[:, hist_cap:]).reshape(n_dest * cand_cap, d_model)
    hist_emb = jnp.dot(hist_pick, hist_replies, preferred_element_type=jnp.float32).astype(jnp.bfloat16)
    cand_emb = jnp.dot(cand_pick, cand_replies, preferred_element_type=jnp.float32).astype(jnp.bfloat16)
    head_size = d_model // HEADS
    scale_factor = 1.0 / math.sqrt(head_size)
    length = history_length[0]
    w_pair = jnp.concatenate([w_key, w_value], axis=1)
    query_row_matrix = jnp.dot(cand_emb, w_query, preferred_element_type=jnp.float32).astype(
        jnp.bfloat16
    )
    query_row_matrix = query_row_matrix.reshape(cand_dev, HEADS, head_size)
    (mine, mine_sources), (partner, partner_sources) = gather_over_cand(hist_emb)
    weighted_sum = attend(
        query_row_matrix,
        jnp.concatenate([mine, partner], axis=0),
        jnp.concatenate([mine_sources, partner_sources]),
        w_pair,
        length,
        scale_factor,
    )
    attended = (
        (weighted_sum / jnp.sqrt(length.astype(jnp.float32)))
        .reshape(cand_dev, d_model)
        .astype(jnp.bfloat16)
    )
    pre_act = jnp.dot(cand_emb, tower_in[:d_model], preferred_element_type=jnp.float32) + jnp.dot(
        attended, tower_in[d_model:], preferred_element_type=jnp.float32
    )
    hidden = (pre_act * logistic(pre_act)).astype(jnp.bfloat16)
    return jnp.dot(hidden, tower_out, preferred_element_type=jnp.float32)[None, :]


def solution(mesh):
    placed = (
        P("req", None),
        P("req", "cand", None),
        P("req", "cand"),
        P("req", "cand", None),
        P("req", "cand"),
        P("req"),
        P(),
        P(),
        P(),
        P(),
        P(),
    )
    return jax.shard_map(
        body, mesh=mesh, in_specs=placed, out_specs=P("req", "cand"), check_vma=False
    )
```

```python
import math

import jax
import jax.numpy as jnp
from jax import lax
from jax.sharding import PartitionSpec as P

HEADS = 4


def slot_index(shard_ids, slot_count):
    count = shard_ids.shape[0]
    earlier = lax.broadcasted_iota(jnp.int32, (count, count), 1) < lax.broadcasted_iota(
        jnp.int32, (count, count), 0
    )
    same = (shard_ids[:, None] == shard_ids[None, :]) & earlier
    rank = jnp.sum(same.astype(jnp.int32), axis=1)
    return shard_ids * slot_count + rank


def select_rows(slots, n_slots):
    return (slots[:, None] == lax.broadcasted_iota(jnp.int32, (slots.shape[0], n_slots), 1)).astype(
        jnp.bfloat16
    )


def gather_over_cand(rows):
    n_cand = lax.axis_size("cand")
    assert n_cand & (n_cand - 1) == 0
    me = lax.axis_index("cand")
    blocks, sources = [rows], [me]
    for hop in range(2, n_cand, 2):
        blocks.append(lax.ppermute(rows, "cand", [(i, i ^ hop) for i in range(n_cand)]))
        sources.append(me ^ hop)
    forwarded = [lax.ppermute(block, "cand", [(i, i ^ 1) for i in range(n_cand)]) for block in blocks]
    source = jnp.stack(sources)
    return (jnp.stack(blocks, axis=0), source), (jnp.stack(forwarded, axis=0), source ^ 1)


def logistic(x):
    return 0.5 + 0.5 * jnp.tanh(0.5 * x)


def attend(query, blocks, sources, w_pair, length, scale_factor):
    n_blocks, block_rows, d_model = blocks.shape
    count = n_blocks * block_rows
    head_size = d_model // HEADS
    pair_rows = jnp.dot(
        blocks.reshape(count, d_model), w_pair, preferred_element_type=jnp.float32
    ).astype(jnp.bfloat16)
    keys = pair_rows[:, :d_model].reshape(count, HEADS, head_size)
    values = pair_rows[:, d_model:].reshape(count, HEADS, head_size)
    scores = jnp.einsum("zun,aun->zua", query, keys, preferred_element_type=jnp.float32) * scale_factor
    position = (sources[:, None] * block_rows + jnp.arange(block_rows, dtype=jnp.int32)[None, :]).reshape(
        count
    )
    gates = jnp.where(
        (position < length)[None, None, :], logistic(scores), jnp.float32(0.0)
    ).astype(jnp.bfloat16)
    return jnp.einsum("bgo,ogl->bgl", gates, values, preferred_element_type=jnp.float32)


def wanted_rows(slots, n_slots, rows):
    pick_t = (lax.broadcasted_iota(jnp.int32, (n_slots, slots.shape[0]), 0) == slots[None, :]).astype(
        jnp.bfloat16
    )
    row_parts = jnp.stack([rows // 128, rows % 128], axis=1).astype(jnp.bfloat16)
    parts = jnp.dot(pick_t, row_parts, preferred_element_type=jnp.float32).astype(jnp.int32)
    return parts[:, 0] * 128 + parts[:, 1]


def swap_over_req(blocks):
    n_req = blocks.shape[0]
    swapped = [blocks[0]]
    for hop in range(1, n_req):
        swapped.append(lax.ppermute(blocks[hop], "req", [(i, i ^ hop) for i in range(n_req)]))
    return jnp.stack(swapped, axis=0)


def body(
    table,
    history_shard,
    history_row,
    candidate_shard,
    candidate_row,
    history_length,
    w_query,
    w_key,
    w_value,
    tower_in,
    tower_out,
):
    n_dest = lax.axis_size("req")
    d_model = table.shape[1]
    hist_dev = history_row.shape[1]
    cand_dev = candidate_row.shape[1]
    packed = lax.optimization_barrier(
        jnp.concatenate(
            [history_shard[0, :, 0], history_row[0], candidate_shard[0, :, 0], candidate_row[0]]
        )
    )
    hist_shards = packed[:hist_dev]
    hist_rows = packed[hist_dev : 2 * hist_dev]
    cand_shards = packed[2 * hist_dev : 2 * hist_dev + cand_dev]
    cand_rows = packed[2 * hist_dev + cand_dev :]
    hist_cap = 4 * hist_dev // n_dest
    cand_cap = 3 * cand_dev // n_dest
    assert n_dest & (n_dest - 1) == 0
    me = lax.axis_index("req")
    hist_slot = slot_index(hist_shards ^ me, hist_cap)
    cand_slot = slot_index(cand_shards ^ me, cand_cap)
    hist_pick = select_rows(hist_slot, n_dest * hist_cap)
    cand_pick = select_rows(cand_slot, n_dest * cand_cap)
    hist_wanted = wanted_rows(hist_slot, n_dest * hist_cap, hist_rows).reshape(n_dest, hist_cap)
    cand_wanted = wanted_rows(cand_slot, n_dest * cand_cap, cand_rows).reshape(n_dest, cand_cap)
    asked = swap_over_req(jnp.concatenate([hist_wanted, cand_wanted], axis=1))
    fetched = jnp.take(table, asked.reshape(-1), axis=0, mode="clip").reshape(
        n_dest, hist_cap + cand_cap, d_model
    )
    hist_replies = swap_over_req(fetched[:, :hist_cap]).reshape(n_dest * hist_cap, d_model)
    cand_replies = swap_over_req(fetched[:, hist_cap:]).reshape(n_dest * cand_cap, d_model)
    hist_emb = jnp.dot(hist_pick, hist_replies, preferred_element_type=jnp.float32).astype(jnp.bfloat16)
    cand_emb = jnp.dot(cand_pick, cand_replies, preferred_element_type=jnp.float32).astype(jnp.bfloat16)
    head_size = d_model // HEADS
    scale_factor = 1.0 / math.sqrt(head_size)
    length = history_length[0]
    w_pair = jnp.concatenate([w_key, w_value], axis=1)
    query_row_matrix = jnp.dot(cand_emb, w_query, preferred_element_type=jnp.float32).astype(
        jnp.bfloat16
    )
    query_row_matrix = query_row_matrix.reshape(cand_dev, HEADS, head_size)
    (mine, mine_sources), (partner, partner_sources) = gather_over_cand(hist_emb)
    weighted_sum = attend(
        query_row_matrix,
        jnp.concatenate([mine, partner], axis=0),
        jnp.concatenate([mine_sources, partner_sources]),
        w_pair,
        length,
        scale_factor,
    )
    attended = (
        (weighted_sum / jnp.sqrt(length.astype(jnp.float32)))
        .reshape(cand_dev, d_model)
        .astype(jnp.bfloat16)
    )
    pre_act = jnp.dot(cand_emb, tower_in[:d_model], preferred_element_type=jnp.float32) + jnp.dot(
        attended, tower_in[d_model:], preferred_element_type=jnp.float32
    )
    hidden = (pre_act * logistic(pre_act)).astype(jnp.bfloat16)
    return jnp.dot(hidden, tower_out, preferred_element_type=jnp.float32)[None, :]


def solution(mesh):
    placed = (
        P("req", None),
        P("req", "cand", None),
        P("req", "cand"),
        P("req", "cand", None),
        P("req", "cand"),
        P("req"),
        P(),
        P(),
        P(),
        P(),
        P(),
    )
    return jax.shard_map(
        body, mesh=mesh, in_specs=placed, out_specs=P("req", "cand"), check_vma=False
    )
```

```python
import math

import jax
import jax.numpy as jnp
from jax import lax
from jax.sharding import PartitionSpec as P

HEADS = 4


def slot_index(shard_ids, slot_count):
    count = shard_ids.shape[0]
    earlier = lax.broadcasted_iota(jnp.int32, (count, count), 1) < lax.broadcasted_iota(
        jnp.int32, (count, count), 0
    )
    same = (shard_ids[:, None] == shard_ids[None, :]) & earlier
    rank = jnp.sum(same.astype(jnp.int32), axis=1)
    return shard_ids * slot_count + rank


def select_rows(slots, n_slots):
    return (slots[:, None] == lax.broadcasted_iota(jnp.int32, (slots.shape[0], n_slots), 1)).astype(
        jnp.bfloat16
    )


def gather_over_cand(rows):
    n_cand = lax.axis_size("cand")
    assert n_cand & (n_cand - 1) == 0
    me = lax.axis_index("cand")
    blocks, sources = [rows], [me]
    for hop in range(2, n_cand, 2):
        blocks.append(lax.ppermute(rows, "cand", [(i, i ^ hop) for i in range(n_cand)]))
        sources.append(me ^ hop)
    forwarded = [lax.ppermute(block, "cand", [(i, i ^ 1) for i in range(n_cand)]) for block in blocks]
    source = jnp.stack(sources)
    return (jnp.stack(blocks, axis=0), source), (jnp.stack(forwarded, axis=0), source ^ 1)


def logistic(x):
    return 0.5 + 0.5 * jnp.tanh(0.5 * x)


def attend(query, blocks, sources, w_pair, length, scale_factor):
    n_blocks, block_rows, d_model = blocks.shape
    count = n_blocks * block_rows
    head_size = d_model // HEADS
    pair_rows = jnp.dot(
        blocks.reshape(count, d_model), w_pair, preferred_element_type=jnp.float32
    ).astype(jnp.bfloat16)
    keys = pair_rows[:, :d_model].reshape(count, HEADS, head_size)
    values = pair_rows[:, d_model:].reshape(count, HEADS, head_size)
    scores = jnp.einsum("zun,aun->zua", query, keys, preferred_element_type=jnp.float32) * scale_factor
    position = (sources[:, None] * block_rows + jnp.arange(block_rows, dtype=jnp.int32)[None, :]).reshape(
        count
    )
    gates = jnp.where(
        (position < length)[None, None, :], logistic(scores), jnp.float32(0.0)
    ).astype(jnp.bfloat16)
    return jnp.einsum("bgo,ogl->bgl", gates, values, preferred_element_type=jnp.float32)


def wanted_rows(slots, n_slots, rows):
    pick_t = (lax.broadcasted_iota(jnp.int32, (n_slots, slots.shape[0]), 0) == slots[None, :]).astype(
        jnp.bfloat16
    )
    row_parts = jnp.stack([rows // 128, rows % 128], axis=1).astype(jnp.bfloat16)
    parts = jnp.dot(pick_t, row_parts, preferred_element_type=jnp.float32).astype(jnp.int32)
    return parts[:, 0] * 128 + parts[:, 1]


def swap_over_req(blocks):
    n_req = blocks.shape[0]
    swapped = [blocks[0]]
    for hop in range(1, n_req):
        swapped.append(lax.ppermute(blocks[hop], "req", [(i, i ^ hop) for i in range(n_req)]))
    return jnp.stack(swapped, axis=0)


def body(
    table,
    history_shard,
    history_row,
    candidate_shard,
    candidate_row,
    history_length,
    w_query,
    w_key,
    w_value,
    tower_in,
    tower_out,
):
    n_dest = lax.axis_size("req")
    d_model = table.shape[1]
    hist_dev = history_row.shape[1]
    cand_dev = candidate_row.shape[1]
    packed = lax.optimization_barrier(
        jnp.concatenate(
            [history_shard[0, :, 0], history_row[0], candidate_shard[0, :, 0], candidate_row[0]]
        )
    )
    hist_shards = packed[:hist_dev]
    hist_rows = packed[hist_dev : 2 * hist_dev]
    cand_shards = packed[2 * hist_dev : 2 * hist_dev + cand_dev]
    cand_rows = packed[2 * hist_dev + cand_dev :]
    hist_cap = 4 * hist_dev // n_dest
    cand_cap = 3 * cand_dev // n_dest
    assert n_dest & (n_dest - 1) == 0
    me = lax.axis_index("req")
    hist_slot = slot_index(hist_shards ^ me, hist_cap)
    cand_slot = slot_index(cand_shards ^ me, cand_cap)
    hist_pick = select_rows(hist_slot, n_dest * hist_cap)
    cand_pick = select_rows(cand_slot, n_dest * cand_cap)
    hist_wanted = wanted_rows(hist_slot, n_dest * hist_cap, hist_rows).reshape(n_dest, hist_cap)
    cand_wanted = wanted_rows(cand_slot, n_dest * cand_cap, cand_rows).reshape(n_dest, cand_cap)
    asked = swap_over_req(jnp.concatenate([hist_wanted, cand_wanted], axis=1))
    fetched = jnp.take(table, asked.reshape(-1), axis=0, mode="clip").reshape(
        n_dest, hist_cap + cand_cap, d_model
    )
    hist_replies = swap_over_req(fetched[:, :hist_cap]).reshape(n_dest * hist_cap, d_model)
    hist_emb = jnp.dot(hist_pick, hist_replies, preferred_element_type=jnp.float32).astype(jnp.bfloat16)
    cand_sent, hist_emb = lax.optimization_barrier((fetched[:, hist_cap:], hist_emb))
    cand_replies = swap_over_req(cand_sent).reshape(n_dest * cand_cap, d_model)
    cand_emb = jnp.dot(cand_pick, cand_replies, preferred_element_type=jnp.float32).astype(jnp.bfloat16)
    head_size = d_model // HEADS
    scale_factor = 1.0 / math.sqrt(head_size)
    length = history_length[0]
    w_pair = jnp.concatenate([w_key, w_value], axis=1)
    query_row_matrix = jnp.dot(cand_emb, w_query, preferred_element_type=jnp.float32).astype(
        jnp.bfloat16
    )
    query_row_matrix = query_row_matrix.reshape(cand_dev, HEADS, head_size)
    (mine, mine_sources), (partner, partner_sources) = gather_over_cand(hist_emb)
    weighted_sum = attend(
        query_row_matrix,
        jnp.concatenate([mine, partner], axis=0),
        jnp.concatenate([mine_sources, partner_sources]),
        w_pair,
        length,
        scale_factor,
    )
    attended = (
        (weighted_sum / jnp.sqrt(length.astype(jnp.float32)))
        .reshape(cand_dev, d_model)
        .astype(jnp.bfloat16)
    )
    pre_act = jnp.dot(cand_emb, tower_in[:d_model], preferred_element_type=jnp.float32) + jnp.dot(
        attended, tower_in[d_model:], preferred_element_type=jnp.float32
    )
    hidden = (pre_act * logistic(pre_act)).astype(jnp.bfloat16)
    return jnp.dot(hidden, tower_out, preferred_element_type=jnp.float32)[None, :]


def solution(mesh):
    placed = (
        P("req", None),
        P("req", "cand", None),
        P("req", "cand"),
        P("req", "cand", None),
        P("req", "cand"),
        P("req"),
        P(),
        P(),
        P(),
        P(),
        P(),
    )
    return jax.shard_map(
        body, mesh=mesh, in_specs=placed, out_specs=P("req", "cand"), check_vma=False
    )
```

```python
import math

import jax
import jax.numpy as jnp
from jax import lax
from jax.sharding import PartitionSpec as P

HEADS = 4


def slot_index(shard_ids, slot_count):
    count = shard_ids.shape[0]
    earlier = lax.broadcasted_iota(jnp.int32, (count, count), 1) < lax.broadcasted_iota(
        jnp.int32, (count, count), 0
    )
    same = (shard_ids[:, None] == shard_ids[None, :]) & earlier
    rank = jnp.sum(same.astype(jnp.int32), axis=1)
    return shard_ids * slot_count + rank


def select_rows(slots, n_slots):
    return (slots[:, None] == lax.broadcasted_iota(jnp.int32, (slots.shape[0], n_slots), 1)).astype(
        jnp.bfloat16
    )


def gather_over_cand(rows):
    n_cand = lax.axis_size("cand")
    assert n_cand & (n_cand - 1) == 0
    me = lax.axis_index("cand")
    blocks, sources = [rows], [me]
    for hop in range(2, n_cand, 2):
        blocks.append(lax.ppermute(rows, "cand", [(i, i ^ hop) for i in range(n_cand)]))
        sources.append(me ^ hop)
    forwarded = [lax.ppermute(block, "cand", [(i, i ^ 1) for i in range(n_cand)]) for block in blocks]
    source = jnp.stack(sources)
    return (jnp.stack(blocks, axis=0), source), (jnp.stack(forwarded, axis=0), source ^ 1)


def logistic(x):
    return 0.5 + 0.5 * jnp.tanh(0.5 * x)


def attend(query, blocks, sources, w_pair, length, scale_factor):
    n_blocks, block_rows, d_model = blocks.shape
    count = n_blocks * block_rows
    head_size = d_model // HEADS
    pair_rows = jnp.dot(
        blocks.reshape(count, d_model), w_pair, preferred_element_type=jnp.float32
    ).astype(jnp.bfloat16)
    keys = pair_rows[:, :d_model].reshape(count, HEADS, head_size)
    values = pair_rows[:, d_model:].reshape(count, HEADS, head_size)
    scores = jnp.einsum("zun,aun->uza", query, keys, preferred_element_type=jnp.float32) * scale_factor
    position = (sources[:, None] * block_rows + jnp.arange(block_rows, dtype=jnp.int32)[None, :]).reshape(
        count
    )
    gates = jnp.where(
        (position < length)[None, None, :], logistic(scores), jnp.float32(0.0)
    ).astype(jnp.bfloat16)
    return jnp.einsum("gbo,ogl->bgl", gates, values, preferred_element_type=jnp.float32)


def wanted_rows(slots, n_slots, rows):
    pick_t = (lax.broadcasted_iota(jnp.int32, (n_slots, slots.shape[0]), 0) == slots[None, :]).astype(
        jnp.bfloat16
    )
    row_parts = jnp.stack([rows // 128, rows % 128], axis=1).astype(jnp.bfloat16)
    parts = jnp.dot(pick_t, row_parts, preferred_element_type=jnp.float32).astype(jnp.int32)
    return parts[:, 0] * 128 + parts[:, 1]


def swap_over_req(blocks):
    n_req = blocks.shape[0]
    swapped = [blocks[0]]
    for hop in range(1, n_req):
        swapped.append(lax.ppermute(blocks[hop], "req", [(i, i ^ hop) for i in range(n_req)]))
    return jnp.stack(swapped, axis=0)


def body(
    table,
    history_shard,
    history_row,
    candidate_shard,
    candidate_row,
    history_length,
    w_query,
    w_key,
    w_value,
    tower_in,
    tower_out,
):
    n_dest = lax.axis_size("req")
    d_model = table.shape[1]
    hist_dev = history_row.shape[1]
    cand_dev = candidate_row.shape[1]
    packed = lax.optimization_barrier(
        jnp.concatenate(
            [history_shard[0, :, 0], history_row[0], candidate_shard[0, :, 0], candidate_row[0]]
        )
    )
    hist_shards = packed[:hist_dev]
    hist_rows = packed[hist_dev : 2 * hist_dev]
    cand_shards = packed[2 * hist_dev : 2 * hist_dev + cand_dev]
    cand_rows = packed[2 * hist_dev + cand_dev :]
    hist_cap = 4 * hist_dev // n_dest
    cand_cap = 3 * cand_dev // n_dest
    assert n_dest & (n_dest - 1) == 0
    me = lax.axis_index("req")
    hist_slot = slot_index(hist_shards ^ me, hist_cap)
    cand_slot = slot_index(cand_shards ^ me, cand_cap)
    hist_pick = select_rows(hist_slot, n_dest * hist_cap)
    cand_pick = select_rows(cand_slot, n_dest * cand_cap)
    hist_wanted = wanted_rows(hist_slot, n_dest * hist_cap, hist_rows).reshape(n_dest, hist_cap)
    cand_wanted = wanted_rows(cand_slot, n_dest * cand_cap, cand_rows).reshape(n_dest, cand_cap)
    asked = swap_over_req(jnp.concatenate([hist_wanted, cand_wanted], axis=1))
    fetched = jnp.take(table, asked.reshape(-1), axis=0, mode="clip").reshape(
        n_dest, hist_cap + cand_cap, d_model
    )
    hist_replies = swap_over_req(fetched[:, :hist_cap]).reshape(n_dest * hist_cap, d_model)
    cand_replies = swap_over_req(fetched[:, hist_cap:]).reshape(n_dest * cand_cap, d_model)
    hist_emb = jnp.dot(hist_pick, hist_replies, preferred_element_type=jnp.float32).astype(jnp.bfloat16)
    cand_emb = jnp.dot(cand_pick, cand_replies, preferred_element_type=jnp.float32).astype(jnp.bfloat16)
    head_size = d_model // HEADS
    scale_factor = 1.0 / math.sqrt(head_size)
    length = history_length[0]
    w_pair = jnp.concatenate([w_key, w_value], axis=1)
    query_row_matrix = jnp.dot(cand_emb, w_query, preferred_element_type=jnp.float32).astype(
        jnp.bfloat16
    )
    query_row_matrix = query_row_matrix.reshape(cand_dev, HEADS, head_size)
    (mine, mine_sources), (partner, partner_sources) = gather_over_cand(hist_emb)
    weighted_sum = attend(
        query_row_matrix,
        jnp.concatenate([mine, partner], axis=0),
        jnp.concatenate([mine_sources, partner_sources]),
        w_pair,
        length,
        scale_factor,
    )
    attended = (
        (weighted_sum / jnp.sqrt(length.astype(jnp.float32)))
        .reshape(cand_dev, d_model)
        .astype(jnp.bfloat16)
    )
    pre_act = jnp.dot(cand_emb, tower_in[:d_model], preferred_element_type=jnp.float32) + jnp.dot(
        attended, tower_in[d_model:], preferred_element_type=jnp.float32
    )
    hidden = (pre_act * logistic(pre_act)).astype(jnp.bfloat16)
    return jnp.dot(hidden, tower_out, preferred_element_type=jnp.float32)[None, :]


def solution(mesh):
    placed = (
        P("req", None),
        P("req", "cand", None),
        P("req", "cand"),
        P("req", "cand", None),
        P("req", "cand"),
        P("req"),
        P(),
        P(),
        P(),
        P(),
        P(),
    )
    return jax.shard_map(
        body, mesh=mesh, in_specs=placed, out_specs=P("req", "cand"), check_vma=False
    )
```

```python
import math

import jax
import jax.numpy as jnp
from jax import lax
from jax.sharding import PartitionSpec as P

HEADS = 4


def slot_index(shard_ids, slot_count):
    count = shard_ids.shape[0]
    earlier = lax.broadcasted_iota(jnp.int32, (count, count), 1) < lax.broadcasted_iota(
        jnp.int32, (count, count), 0
    )
    same = (shard_ids[:, None] == shard_ids[None, :]) & earlier
    rank = jnp.sum(same.astype(jnp.int32), axis=1)
    return shard_ids * slot_count + rank


def select_rows(slots, n_slots):
    return (slots[:, None] == lax.broadcasted_iota(jnp.int32, (slots.shape[0], n_slots), 1)).astype(
        jnp.bfloat16
    )


def gather_over_cand(rows):
    n_cand = lax.axis_size("cand")
    assert n_cand & (n_cand - 1) == 0
    me = lax.axis_index("cand")
    blocks, sources = [rows], [me]
    for hop in range(2, n_cand, 2):
        blocks.append(lax.ppermute(rows, "cand", [(i, i ^ hop) for i in range(n_cand)]))
        sources.append(me ^ hop)
    forwarded = [lax.ppermute(block, "cand", [(i, i ^ 1) for i in range(n_cand)]) for block in blocks]
    source = jnp.stack(sources)
    return (jnp.stack(blocks, axis=0), source), (jnp.stack(forwarded, axis=0), source ^ 1)


def logistic(x):
    return 0.5 + 0.5 * jnp.tanh(0.5 * x)


def attend(query, blocks, sources, w_pair, length, scale_factor):
    n_blocks, block_rows, d_model = blocks.shape
    count = n_blocks * block_rows
    head_size = d_model // HEADS
    pair_rows = jnp.dot(
        blocks.reshape(count, d_model), w_pair, preferred_element_type=jnp.float32
    ).astype(jnp.bfloat16)
    keys = pair_rows[:, :d_model].reshape(count, HEADS, head_size)
    values = pair_rows[:, d_model:].reshape(count, HEADS, head_size)
    scores = jnp.einsum("zun,aun->zua", query, keys, preferred_element_type=jnp.float32) * scale_factor
    position = (sources[:, None] * block_rows + jnp.arange(block_rows, dtype=jnp.int32)[None, :]).reshape(
        count
    )
    gates = jnp.where(
        (position < length)[None, None, :], logistic(scores), jnp.float32(0.0)
    ).astype(jnp.bfloat16)
    return jnp.einsum("bgo,ogl->bgl", gates, values, preferred_element_type=jnp.float32)


def wanted_rows(slots, n_slots, rows):
    pick_t = (lax.broadcasted_iota(jnp.int32, (n_slots, slots.shape[0]), 0) == slots[None, :]).astype(
        jnp.bfloat16
    )
    row_parts = jnp.stack([rows // 128, rows % 128], axis=1).astype(jnp.bfloat16)
    parts = jnp.dot(pick_t, row_parts, preferred_element_type=jnp.float32).astype(jnp.int32)
    return parts[:, 0] * 128 + parts[:, 1]


def swap_over_req(blocks):
    n_req = blocks.shape[0]
    swapped = [blocks[0]]
    for hop in range(1, n_req):
        swapped.append(lax.ppermute(blocks[hop], "req", [(i, i ^ hop) for i in range(n_req)]))
    return jnp.stack(swapped, axis=0)


def body(
    table,
    history_shard,
    history_row,
    candidate_shard,
    candidate_row,
    history_length,
    w_query,
    w_key,
    w_value,
    tower_in,
    tower_out,
):
    n_dest = lax.axis_size("req")
    d_model = table.shape[1]
    hist_dev = history_row.shape[1]
    cand_dev = candidate_row.shape[1]
    packed = lax.optimization_barrier(
        jnp.concatenate(
            [history_shard[0, :, 0], history_row[0], candidate_shard[0, :, 0], candidate_row[0]]
        )
    )
    hist_shards = packed[:hist_dev]
    hist_rows = packed[hist_dev : 2 * hist_dev]
    cand_shards = packed[2 * hist_dev : 2 * hist_dev + cand_dev]
    cand_rows = packed[2 * hist_dev + cand_dev :]
    hist_cap = 4 * hist_dev // n_dest
    cand_cap = 3 * cand_dev // n_dest
    assert n_dest & (n_dest - 1) == 0
    me = lax.axis_index("req")
    hist_slot = slot_index(hist_shards ^ me, hist_cap)
    cand_slot = slot_index(cand_shards ^ me, cand_cap)
    hist_pick = select_rows(hist_slot, n_dest * hist_cap)
    cand_pick = select_rows(cand_slot, n_dest * cand_cap)
    hist_wanted = wanted_rows(hist_slot, n_dest * hist_cap, hist_rows).reshape(n_dest, hist_cap)
    cand_wanted = wanted_rows(cand_slot, n_dest * cand_cap, cand_rows).reshape(n_dest, cand_cap)
    asked = swap_over_req(jnp.concatenate([hist_wanted, cand_wanted], axis=1))
    fetched = jnp.take(table, asked.reshape(-1), axis=0, mode="clip").reshape(
        n_dest, hist_cap + cand_cap, d_model
    )
    hist_replies = swap_over_req(fetched[:, :hist_cap]).reshape(n_dest * hist_cap, d_model)
    cand_replies = swap_over_req(fetched[:, hist_cap:]).reshape(n_dest * cand_cap, d_model)
    hist_emb = jnp.dot(hist_pick, hist_replies, preferred_element_type=jnp.float32).astype(jnp.bfloat16)
    cand_emb = jnp.dot(cand_pick, cand_replies, preferred_element_type=jnp.float32).astype(jnp.bfloat16)
    head_size = d_model // HEADS
    scale_factor = 1.0 / math.sqrt(head_size)
    length = history_length[0]
    w_pair = jnp.concatenate([w_key, w_value], axis=1)
    query_row_matrix = jnp.dot(cand_emb, w_query, preferred_element_type=jnp.float32).astype(
        jnp.bfloat16
    )
    query_row_matrix = query_row_matrix.reshape(cand_dev, HEADS, head_size)
    (mine, mine_sources), (partner, partner_sources) = gather_over_cand(hist_emb)
    weighted_sum = attend(
        query_row_matrix,
        jnp.concatenate([mine, partner], axis=0),
        jnp.concatenate([mine_sources, partner_sources]),
        w_pair,
        length,
        scale_factor,
    )
    attended = (
        (weighted_sum / jnp.sqrt(length.astype(jnp.float32)))
        .reshape(cand_dev, d_model)
        .astype(jnp.bfloat16)
    )
    pre_act = jnp.dot(cand_emb, tower_in[:d_model], preferred_element_type=jnp.float32) + jnp.dot(
        attended, tower_in[d_model:], preferred_element_type=jnp.float32
    )
    hidden = (pre_act * logistic(pre_act)).astype(jnp.bfloat16)
    products = hidden.astype(jnp.float32) * tower_out.astype(jnp.float32)[None, :]
    return jnp.sum(products, axis=1)[None, :]


def solution(mesh):
    placed = (
        P("req", None),
        P("req", "cand", None),
        P("req", "cand"),
        P("req", "cand", None),
        P("req", "cand"),
        P("req"),
        P(),
        P(),
        P(),
        P(),
        P(),
    )
    return jax.shard_map(
        body, mesh=mesh, in_specs=placed, out_specs=P("req", "cand"), check_vma=False
    )
```

```python
import math

import jax
import jax.numpy as jnp
from jax import lax
from jax.sharding import PartitionSpec as P

HEADS = 4


def slot_index(shard_ids, slot_count):
    count = shard_ids.shape[0]
    earlier = lax.broadcasted_iota(jnp.int32, (count, count), 1) < lax.broadcasted_iota(
        jnp.int32, (count, count), 0
    )
    same = (shard_ids[:, None] == shard_ids[None, :]) & earlier
    rank = jnp.sum(same.astype(jnp.int32), axis=1)
    return shard_ids * slot_count + rank


def select_rows(slots, n_slots):
    return (slots[:, None] == lax.broadcasted_iota(jnp.int32, (slots.shape[0], n_slots), 1)).astype(
        jnp.bfloat16
    )


def gather_over_cand(rows):
    n_cand = lax.axis_size("cand")
    assert n_cand & (n_cand - 1) == 0
    me = lax.axis_index("cand")
    blocks, sources = [rows], [me]
    for hop in range(2, n_cand, 2):
        blocks.append(lax.ppermute(rows, "cand", [(i, i ^ hop) for i in range(n_cand)]))
        sources.append(me ^ hop)
    forwarded = [lax.ppermute(block, "cand", [(i, i ^ 1) for i in range(n_cand)]) for block in blocks]
    source = jnp.stack(sources)
    return (jnp.stack(blocks, axis=0), source), (jnp.stack(forwarded, axis=0), source ^ 1)


def logistic(x):
    return 0.5 + 0.5 * jnp.tanh(0.5 * x)


def project(blocks, w_pair):
    n_blocks, block_rows, d_model = blocks.shape
    return jnp.dot(
        blocks.reshape(n_blocks * block_rows, d_model), w_pair, preferred_element_type=jnp.float32
    ).astype(jnp.bfloat16)


def attend(query, pair_rows, sources, block_rows, length, scale_factor):
    count, d_model = pair_rows.shape[0], pair_rows.shape[1] // 2
    head_size = d_model // HEADS
    keys = pair_rows[:, :d_model].reshape(count, HEADS, head_size)
    values = pair_rows[:, d_model:].reshape(count, HEADS, head_size)
    scores = jnp.einsum("zun,aun->zua", query, keys, preferred_element_type=jnp.float32) * scale_factor
    position = (sources[:, None] * block_rows + jnp.arange(block_rows, dtype=jnp.int32)[None, :]).reshape(
        count
    )
    gates = jnp.where(
        (position < length)[None, None, :], logistic(scores), jnp.float32(0.0)
    ).astype(jnp.bfloat16)
    return jnp.einsum("bgo,ogl->bgl", gates, values, preferred_element_type=jnp.float32)


def wanted_rows(slots, n_slots, rows):
    pick_t = (lax.broadcasted_iota(jnp.int32, (n_slots, slots.shape[0]), 0) == slots[None, :]).astype(
        jnp.bfloat16
    )
    row_parts = jnp.stack([rows // 128, rows % 128], axis=1).astype(jnp.bfloat16)
    parts = jnp.dot(pick_t, row_parts, preferred_element_type=jnp.float32).astype(jnp.int32)
    return parts[:, 0] * 128 + parts[:, 1]


def swap_over_req(blocks):
    n_req = blocks.shape[0]
    swapped = [blocks[0]]
    for hop in range(1, n_req):
        swapped.append(lax.ppermute(blocks[hop], "req", [(i, i ^ hop) for i in range(n_req)]))
    return jnp.stack(swapped, axis=0)


def body(
    table,
    history_shard,
    history_row,
    candidate_shard,
    candidate_row,
    history_length,
    w_query,
    w_key,
    w_value,
    tower_in,
    tower_out,
):
    n_dest = lax.axis_size("req")
    d_model = table.shape[1]
    hist_dev = history_row.shape[1]
    cand_dev = candidate_row.shape[1]
    packed = lax.optimization_barrier(
        jnp.concatenate(
            [history_shard[0, :, 0], history_row[0], candidate_shard[0, :, 0], candidate_row[0]]
        )
    )
    hist_shards = packed[:hist_dev]
    hist_rows = packed[hist_dev : 2 * hist_dev]
    cand_shards = packed[2 * hist_dev : 2 * hist_dev + cand_dev]
    cand_rows = packed[2 * hist_dev + cand_dev :]
    hist_cap = 4 * hist_dev // n_dest
    cand_cap = 3 * cand_dev // n_dest
    assert n_dest & (n_dest - 1) == 0
    me = lax.axis_index("req")
    hist_slot = slot_index(hist_shards ^ me, hist_cap)
    cand_slot = slot_index(cand_shards ^ me, cand_cap)
    hist_pick = select_rows(hist_slot, n_dest * hist_cap)
    cand_pick = select_rows(cand_slot, n_dest * cand_cap)
    hist_wanted = wanted_rows(hist_slot, n_dest * hist_cap, hist_rows).reshape(n_dest, hist_cap)
    cand_wanted = wanted_rows(cand_slot, n_dest * cand_cap, cand_rows).reshape(n_dest, cand_cap)
    asked = swap_over_req(jnp.concatenate([hist_wanted, cand_wanted], axis=1))
    fetched = jnp.take(table, asked.reshape(-1), axis=0, mode="clip").reshape(
        n_dest, hist_cap + cand_cap, d_model
    )
    hist_replies = swap_over_req(fetched[:, :hist_cap]).reshape(n_dest * hist_cap, d_model)
    cand_replies = swap_over_req(fetched[:, hist_cap:]).reshape(n_dest * cand_cap, d_model)
    hist_emb = jnp.dot(hist_pick, hist_replies, preferred_element_type=jnp.float32).astype(jnp.bfloat16)
    cand_emb = jnp.dot(cand_pick, cand_replies, preferred_element_type=jnp.float32).astype(jnp.bfloat16)
    head_size = d_model // HEADS
    scale_factor = 1.0 / math.sqrt(head_size)
    length = history_length[0]
    w_pair = jnp.concatenate([w_key, w_value], axis=1)
    query_row_matrix = jnp.dot(cand_emb, w_query, preferred_element_type=jnp.float32).astype(
        jnp.bfloat16
    )
    query_row_matrix = query_row_matrix.reshape(cand_dev, HEADS, head_size)
    (mine, mine_sources), (partner, partner_sources) = gather_over_cand(hist_emb)
    weighted_sum = attend(
        query_row_matrix,
        jnp.concatenate([project(mine, w_pair), project(partner, w_pair)], axis=0),
        jnp.concatenate([mine_sources, partner_sources]),
        hist_dev,
        length,
        scale_factor,
    )
    attended = (
        (weighted_sum / jnp.sqrt(length.astype(jnp.float32)))
        .reshape(cand_dev, d_model)
        .astype(jnp.bfloat16)
    )
    pre_act = jnp.dot(cand_emb, tower_in[:d_model], preferred_element_type=jnp.float32) + jnp.dot(
        attended, tower_in[d_model:], preferred_element_type=jnp.float32
    )
    hidden = (pre_act * logistic(pre_act)).astype(jnp.bfloat16)
    return jnp.dot(hidden, tower_out, preferred_element_type=jnp.float32)[None, :]


def solution(mesh):
    placed = (
        P("req", None),
        P("req", "cand", None),
        P("req", "cand"),
        P("req", "cand", None),
        P("req", "cand"),
        P("req"),
        P(),
        P(),
        P(),
        P(),
        P(),
    )
    return jax.shard_map(
        body, mesh=mesh, in_specs=placed, out_specs=P("req", "cand"), check_vma=False
    )
```

```python
import math

import jax
import jax.numpy as jnp
from jax import lax
from jax.sharding import PartitionSpec as P

HEADS = 4


def slot_index(shard_ids, slot_count):
    count = shard_ids.shape[0]
    earlier = lax.broadcasted_iota(jnp.int32, (count, count), 1) < lax.broadcasted_iota(
        jnp.int32, (count, count), 0
    )
    same = (shard_ids[:, None] == shard_ids[None, :]) & earlier
    rank = jnp.sum(same.astype(jnp.int32), axis=1)
    return shard_ids * slot_count + rank


def select_rows(slots, n_slots):
    return (slots[:, None] == lax.broadcasted_iota(jnp.int32, (slots.shape[0], n_slots), 1)).astype(
        jnp.bfloat16
    )


def gather_over_cand(rows):
    n_cand = lax.axis_size("cand")
    assert n_cand & (n_cand - 1) == 0
    me = lax.axis_index("cand")
    blocks, sources = [rows], [me]
    for hop in range(2, n_cand, 2):
        blocks.append(lax.ppermute(rows, "cand", [(i, i ^ hop) for i in range(n_cand)]))
        sources.append(me ^ hop)
    forwarded = [lax.ppermute(block, "cand", [(i, i ^ 1) for i in range(n_cand)]) for block in blocks]
    source = jnp.stack(sources)
    return (jnp.stack(blocks, axis=0), source), (jnp.stack(forwarded, axis=0), source ^ 1)


def logistic(x):
    return 0.5 + 0.5 * jnp.tanh(0.5 * x)


def attend(query, blocks, sources, w_pair, length, scale_factor):
    n_blocks, block_rows, d_model = blocks.shape
    count = n_blocks * block_rows
    head_size = d_model // HEADS
    pair_rows = jnp.dot(
        blocks.reshape(count, d_model), w_pair, preferred_element_type=jnp.float32
    ).astype(jnp.bfloat16)
    keys = pair_rows[:, :d_model].reshape(count, HEADS, head_size)
    values = pair_rows[:, d_model:].reshape(count, HEADS, head_size)
    scores = jnp.einsum("zun,aun->zua", query, keys, preferred_element_type=jnp.float32) * scale_factor
    position = (sources[:, None] * block_rows + jnp.arange(block_rows, dtype=jnp.int32)[None, :]).reshape(
        count
    )
    gates = jnp.where(
        (position < length)[None, None, :], logistic(scores), jnp.float32(0.0)
    ).astype(jnp.bfloat16)
    return jnp.einsum("bgo,ogl->bgl", gates, values, preferred_element_type=jnp.float32)


def wanted_rows(slots, n_slots, rows):
    pick_t = (lax.broadcasted_iota(jnp.int32, (n_slots, slots.shape[0]), 0) == slots[None, :]).astype(
        jnp.bfloat16
    )
    row_parts = jnp.stack([rows // 128, rows % 128], axis=1).astype(jnp.bfloat16)
    parts = jnp.dot(pick_t, row_parts, preferred_element_type=jnp.float32).astype(jnp.int32)
    return parts[:, 0] * 128 + parts[:, 1]


def swap_over_req(blocks):
    n_req = blocks.shape[0]
    swapped = [blocks[0]]
    for hop in range(1, n_req):
        swapped.append(lax.ppermute(blocks[hop], "req", [(i, i ^ hop) for i in range(n_req)]))
    return jnp.stack(swapped, axis=0)


def body(
    table,
    history_shard,
    history_row,
    candidate_shard,
    candidate_row,
    history_length,
    w_query,
    w_key,
    w_value,
    tower_in,
    tower_out,
):
    n_dest = lax.axis_size("req")
    d_model = table.shape[1]
    hist_dev = history_row.shape[1]
    cand_dev = candidate_row.shape[1]
    packed = lax.optimization_barrier(
        jnp.concatenate(
            [history_shard[0, :, 0], history_row[0], candidate_shard[0, :, 0], candidate_row[0]]
        )
    )
    hist_shards = packed[:hist_dev]
    hist_rows = packed[hist_dev : 2 * hist_dev]
    cand_shards = packed[2 * hist_dev : 2 * hist_dev + cand_dev]
    cand_rows = packed[2 * hist_dev + cand_dev :]
    hist_cap = 4 * hist_dev // n_dest
    cand_cap = 3 * cand_dev // n_dest
    assert n_dest & (n_dest - 1) == 0
    me = lax.axis_index("req")
    shards = jnp.concatenate([hist_shards, cand_shards]) ^ me
    in_hist = jnp.arange(hist_dev + cand_dev, dtype=jnp.int32) < hist_dev
    earlier = lax.broadcasted_iota(jnp.int32, (shards.shape[0],) * 2, 1) < lax.broadcasted_iota(
        jnp.int32, (shards.shape[0],) * 2, 0
    )
    same = (shards[:, None] == shards[None, :]) & (in_hist[:, None] == in_hist[None, :]) & earlier
    rank = jnp.sum(same.astype(jnp.int32), axis=1)
    hist_slot = (shards * hist_cap + rank)[:hist_dev]
    cand_slot = (shards * cand_cap + rank)[hist_dev:]
    hist_pick = select_rows(hist_slot, n_dest * hist_cap)
    cand_pick = select_rows(cand_slot, n_dest * cand_cap)
    joint_slot = jnp.concatenate([hist_slot, cand_slot + n_dest * hist_cap])
    joint_wanted = wanted_rows(joint_slot, n_dest * (hist_cap + cand_cap), jnp.concatenate([hist_rows, cand_rows]))
    hist_wanted = joint_wanted[: n_dest * hist_cap].reshape(n_dest, hist_cap)
    cand_wanted = joint_wanted[n_dest * hist_cap :].reshape(n_dest, cand_cap)
    asked = swap_over_req(jnp.concatenate([hist_wanted, cand_wanted], axis=1))
    fetched = jnp.take(table, asked.reshape(-1), axis=0, mode="clip").reshape(
        n_dest, hist_cap + cand_cap, d_model
    )
    hist_replies = swap_over_req(fetched[:, :hist_cap]).reshape(n_dest * hist_cap, d_model)
    cand_replies = swap_over_req(fetched[:, hist_cap:]).reshape(n_dest * cand_cap, d_model)
    hist_emb = jnp.dot(hist_pick, hist_replies, preferred_element_type=jnp.float32).astype(jnp.bfloat16)
    cand_emb = jnp.dot(cand_pick, cand_replies, preferred_element_type=jnp.float32).astype(jnp.bfloat16)
    head_size = d_model // HEADS
    scale_factor = 1.0 / math.sqrt(head_size)
    length = history_length[0]
    w_pair = jnp.concatenate([w_key, w_value], axis=1)
    query_row_matrix = jnp.dot(cand_emb, w_query, preferred_element_type=jnp.float32).astype(
        jnp.bfloat16
    )
    query_row_matrix = query_row_matrix.reshape(cand_dev, HEADS, head_size)
    (mine, mine_sources), (partner, partner_sources) = gather_over_cand(hist_emb)
    weighted_sum = attend(
        query_row_matrix,
        jnp.concatenate([mine, partner], axis=0),
        jnp.concatenate([mine_sources, partner_sources]),
        w_pair,
        length,
        scale_factor,
    )
    attended = (
        (weighted_sum / jnp.sqrt(length.astype(jnp.float32)))
        .reshape(cand_dev, d_model)
        .astype(jnp.bfloat16)
    )
    pre_act = jnp.dot(cand_emb, tower_in[:d_model], preferred_element_type=jnp.float32) + jnp.dot(
        attended, tower_in[d_model:], preferred_element_type=jnp.float32
    )
    hidden = (pre_act * logistic(pre_act)).astype(jnp.bfloat16)
    return jnp.dot(hidden, tower_out, preferred_element_type=jnp.float32)[None, :]


def solution(mesh):
    placed = (
        P("req", None),
        P("req", "cand", None),
        P("req", "cand"),
        P("req", "cand", None),
        P("req", "cand"),
        P("req"),
        P(),
        P(),
        P(),
        P(),
        P(),
    )
    return jax.shard_map(
        body, mesh=mesh, in_specs=placed, out_specs=P("req", "cand"), check_vma=False
    )
```

```python
import math

import jax
import jax.numpy as jnp
from jax import lax
from jax.sharding import PartitionSpec as P

HEADS = 4


def slot_index(shard_ids, slot_count):
    count = shard_ids.shape[0]
    earlier = lax.broadcasted_iota(jnp.int32, (count, count), 1) < lax.broadcasted_iota(
        jnp.int32, (count, count), 0
    )
    same = (shard_ids[:, None] == shard_ids[None, :]) & earlier
    rank = jnp.sum(same.astype(jnp.int32), axis=1)
    return shard_ids * slot_count + rank


def select_rows(slots, n_slots):
    return (slots[:, None] == lax.broadcasted_iota(jnp.int32, (slots.shape[0], n_slots), 1)).astype(
        jnp.bfloat16
    )


def gather_over_cand(rows):
    n_cand = lax.axis_size("cand")
    assert n_cand & (n_cand - 1) == 0
    me = lax.axis_index("cand")
    blocks, sources = [rows], [me]
    for hop in range(2, n_cand, 2):
        blocks.append(lax.ppermute(rows, "cand", [(i, i ^ hop) for i in range(n_cand)]))
        sources.append(me ^ hop)
    forwarded = [lax.ppermute(block, "cand", [(i, i ^ 1) for i in range(n_cand)]) for block in blocks]
    source = jnp.stack(sources)
    return (jnp.stack(blocks, axis=0), source), (jnp.stack(forwarded, axis=0), source ^ 1)


def logistic(x):
    return 0.5 + 0.5 * jnp.tanh(0.5 * x)


def attend(query, pair_blocks, sources, length, scale_factor):
    n_blocks, block_rows, width = pair_blocks.shape
    count, d_model = n_blocks * block_rows, width // 2
    head_size = d_model // HEADS
    pair_rows = pair_blocks.reshape(count, width)
    keys = pair_rows[:, :d_model].reshape(count, HEADS, head_size)
    values = pair_rows[:, d_model:].reshape(count, HEADS, head_size)
    scores = jnp.einsum("zun,aun->zua", query, keys, preferred_element_type=jnp.float32) * scale_factor
    position = (sources[:, None] * block_rows + jnp.arange(block_rows, dtype=jnp.int32)[None, :]).reshape(
        count
    )
    gates = jnp.where(
        (position < length)[None, None, :], logistic(scores), jnp.float32(0.0)
    ).astype(jnp.bfloat16)
    return jnp.einsum("bgo,ogl->bgl", gates, values, preferred_element_type=jnp.float32)


def wanted_rows(slots, n_slots, rows):
    pick_t = (lax.broadcasted_iota(jnp.int32, (n_slots, slots.shape[0]), 0) == slots[None, :]).astype(
        jnp.bfloat16
    )
    row_parts = jnp.stack([rows // 128, rows % 128], axis=1).astype(jnp.bfloat16)
    parts = jnp.dot(pick_t, row_parts, preferred_element_type=jnp.float32).astype(jnp.int32)
    return parts[:, 0] * 128 + parts[:, 1]


def swap_over_req(blocks):
    n_req = blocks.shape[0]
    swapped = [blocks[0]]
    for hop in range(1, n_req):
        swapped.append(lax.ppermute(blocks[hop], "req", [(i, i ^ hop) for i in range(n_req)]))
    return jnp.stack(swapped, axis=0)


def body(
    table,
    history_shard,
    history_row,
    candidate_shard,
    candidate_row,
    history_length,
    w_query,
    w_key,
    w_value,
    tower_in,
    tower_out,
):
    n_dest = lax.axis_size("req")
    d_model = table.shape[1]
    hist_dev = history_row.shape[1]
    cand_dev = candidate_row.shape[1]
    packed = lax.optimization_barrier(
        jnp.concatenate(
            [history_shard[0, :, 0], history_row[0], candidate_shard[0, :, 0], candidate_row[0]]
        )
    )
    hist_shards = packed[:hist_dev]
    hist_rows = packed[hist_dev : 2 * hist_dev]
    cand_shards = packed[2 * hist_dev : 2 * hist_dev + cand_dev]
    cand_rows = packed[2 * hist_dev + cand_dev :]
    hist_cap = 4 * hist_dev // n_dest
    cand_cap = 3 * cand_dev // n_dest
    assert n_dest & (n_dest - 1) == 0
    me = lax.axis_index("req")
    shards = jnp.concatenate([hist_shards, cand_shards]) ^ me
    in_hist = jnp.arange(hist_dev + cand_dev, dtype=jnp.int32) < hist_dev
    earlier = lax.broadcasted_iota(jnp.int32, (shards.shape[0],) * 2, 1) < lax.broadcasted_iota(
        jnp.int32, (shards.shape[0],) * 2, 0
    )
    same = (shards[:, None] == shards[None, :]) & (in_hist[:, None] == in_hist[None, :]) & earlier
    rank = jnp.sum(same.astype(jnp.int32), axis=1)
    hist_slot = (shards * hist_cap + rank)[:hist_dev]
    cand_slot = (shards * cand_cap + rank)[hist_dev:]
    hist_pick = select_rows(hist_slot, n_dest * hist_cap)
    cand_pick = select_rows(cand_slot, n_dest * cand_cap)
    joint_slot = jnp.concatenate([hist_slot, cand_slot + n_dest * hist_cap])
    joint_wanted = wanted_rows(joint_slot, n_dest * (hist_cap + cand_cap), jnp.concatenate([hist_rows, cand_rows]))
    hist_wanted = joint_wanted[: n_dest * hist_cap].reshape(n_dest, hist_cap)
    cand_wanted = joint_wanted[n_dest * hist_cap :].reshape(n_dest, cand_cap)
    asked = swap_over_req(jnp.concatenate([hist_wanted, cand_wanted], axis=1))
    fetched = jnp.take(table, asked.reshape(-1), axis=0, mode="clip").reshape(
        n_dest, hist_cap + cand_cap, d_model
    )
    hist_replies = swap_over_req(fetched[:, :hist_cap]).reshape(n_dest * hist_cap, d_model)
    cand_replies = swap_over_req(fetched[:, hist_cap:]).reshape(n_dest * cand_cap, d_model)
    hist_emb = jnp.dot(hist_pick, hist_replies, preferred_element_type=jnp.float32).astype(jnp.bfloat16)
    cand_emb = jnp.dot(cand_pick, cand_replies, preferred_element_type=jnp.float32).astype(jnp.bfloat16)
    head_size = d_model // HEADS
    scale_factor = 1.0 / math.sqrt(head_size)
    length = history_length[0]
    w_pair = jnp.concatenate([w_key, w_value], axis=1)
    query_row_matrix = jnp.dot(cand_emb, w_query, preferred_element_type=jnp.float32).astype(
        jnp.bfloat16
    )
    query_row_matrix = query_row_matrix.reshape(cand_dev, HEADS, head_size)
    pair_local = jnp.dot(hist_emb, w_pair, preferred_element_type=jnp.float32).astype(jnp.bfloat16)
    (mine, mine_sources), (partner, partner_sources) = gather_over_cand(pair_local)
    weighted_sum = attend(
        query_row_matrix,
        jnp.concatenate([mine, partner], axis=0),
        jnp.concatenate([mine_sources, partner_sources]),
        length,
        scale_factor,
    )
    attended = (
        (weighted_sum / jnp.sqrt(length.astype(jnp.float32)))
        .reshape(cand_dev, d_model)
        .astype(jnp.bfloat16)
    )
    pre_act = jnp.dot(cand_emb, tower_in[:d_model], preferred_element_type=jnp.float32) + jnp.dot(
        attended, tower_in[d_model:], preferred_element_type=jnp.float32
    )
    hidden = (pre_act * logistic(pre_act)).astype(jnp.bfloat16)
    return jnp.dot(hidden, tower_out, preferred_element_type=jnp.float32)[None, :]


def solution(mesh):
    placed = (
        P("req", None),
        P("req", "cand", None),
        P("req", "cand"),
        P("req", "cand", None),
        P("req", "cand"),
        P("req"),
        P(),
        P(),
        P(),
        P(),
        P(),
    )
    return jax.shard_map(
        body, mesh=mesh, in_specs=placed, out_specs=P("req", "cand"), check_vma=False
    )
```
